256 devices in a mesh: win: 8 (over y, core), chan: 32 (over x, z).
Axes of the slice: x: 4, y: 4, z: 8, core: 2. Of those that a mesh axis runs over, the one named last changes fastest.
Arguments:
- traces: float32 [8, 15000, 4096], P('win', None, 'chan'), may hold values from -200 to 200
- pair_blocks: int32 [192, 2], P('chan'), may hold values from -1 to 31, as said below
Outputs:
- stacks: float32 [192, 512, 128], P('chan', 'win')
The draws below stay inside these ranges and needn't reach their ends.
Inputs may be any that keep to these rules, and one draw needn't show every extreme that they name: `pair_blocks`: owner o holds rows o * 6 to (o + 1) * 6 - 1. Each row is a block pair (i, i + d) with 1 <= d <= 3, or (-1, -1) for an empty slot; every block pair with an offset in that range stands in exactly one row; some owner has all 6 of its slots filled.
All inputs are finite; a program needn't handle non-finite values.
Results may differ from the reference program's by a relative error of at most 0.003.
Values may be sent and summed in bfloat16 or wider, within the bound.
No kernel may reach another device: no remote copies, remote signals or barrier semaphores. Data moves between devices by JAX's collectives and lax.ppermute only.
A program may use at most 64 MiB of HBM per device.

```python
import math
import jax
import jax.numpy as jnp
from jax import lax

L = 15000
NB = 512
F_LO = 64
HALF = 32
LAGS = 512
REACH = 3
PMAX = 6
CH_DEV = 128
WINDOWS = 8
BLOCKS = 32
CHANNELS = 4096


tone_count = 6


def draw_traces(key, part):
    keys = jax.random.split(key, 5)
    shape = (WINDOWS, L, CHANNELS)
    noise = jnp.clip(jax.random.normal(keys[0], shape, jnp.float32), -6.0, 6.0)
    freqs = jax.random.randint(keys[1], (WINDOWS, tone_count), F_LO, F_LO + NB)
    phases = jax.random.uniform(keys[2], (WINDOWS, tone_count), jnp.float32, -math.pi, math.pi)
    amps = jax.random.uniform(keys[3], (WINDOWS, tone_count, CHANNELS), jnp.float32, 0.5, 3.0)
    amps = amps * (2600.0 / L) ** 0.5
    times = lax.broadcasted_iota(jnp.int32, (1, L, 1), 1)
    total = noise
    for which in range(tone_count):
        angle = (freqs[:, which][:, None, None] * times % L).astype(jnp.float32) * (2.0 * math.pi / L)
        angle = angle + phases[:, which][:, None, None]
        total = total + amps[:, which][:, None, :] * jnp.cos(angle)
    scales = jnp.exp(jax.random.uniform(keys[4], (WINDOWS, 1, CHANNELS), jnp.float32, 0.0, math.log(10.0)))
    return jnp.clip(scales * total, -200.0, 200.0)


def draw_pair_blocks(key, part):
    blocks = BLOCKS
    reach = REACH
    count = blocks * reach - reach * (reach + 1) // 2
    slots = blocks * PMAX
    first = jnp.concatenate([jnp.arange(blocks - dist, dtype=jnp.int32) for dist in range(1, reach + 1)])
    offset = jnp.concatenate([jnp.full((blocks - dist,), dist, jnp.int32) for dist in range(1, reach + 1)])
    keys = jax.random.split(jax.random.fold_in(key, 11), 3)
    busiest = jax.random.randint(keys[0], (), 0, blocks)
    owners = jnp.arange(slots, dtype=jnp.int32) // PMAX
    scores = jax.random.permutation(keys[1], slots).astype(jnp.int32) + 1
    scores = jnp.where(owners == busiest, 0, scores)
    chosen = jnp.argsort(scores, stable=True)[:count]
    order = jax.random.permutation(keys[2], count).astype(jnp.int32)
    slot_pair = jnp.full((slots,), -1, jnp.int32).at[chosen].set(order)
    valid = slot_pair >= 0
    safe = jnp.maximum(slot_pair, 0)
    left = jnp.where(valid, first[safe], -1)
    right = jnp.where(valid, first[safe] + offset[safe], -1)
    return jnp.stack([left, right], axis=1).astype(jnp.int32)


def setup_inputs(seed: int = 0) -> dict:
    streams_of = jax.random.split(jax.random.key(seed), 3)
    traces = draw_traces(jax.random.fold_in(streams_of[2], 71), 0)
    pair_blocks = draw_pair_blocks(jax.random.fold_in(streams_of[2], 71), 0)
    return {"traces": traces, "pair_blocks": pair_blocks}


def band_tables():
    width = NB + 2 * HALF
    rows = jnp.arange(NB, dtype=jnp.int32)[:, None]
    cols = jnp.arange(width, dtype=jnp.int32)[None, :]
    smoother = jnp.where((cols >= rows) & (cols <= rows + 2 * HALF), 1.0 / (2 * HALF + 1), 0.0).astype(jnp.float32)
    taper = jnp.sin(math.pi * (jnp.arange(NB, dtype=jnp.int32).astype(jnp.float32) + 0.5) / NB)
    bins = F_LO + jnp.arange(NB, dtype=jnp.int32)[None, :]
    lagged = jnp.arange(LAGS, dtype=jnp.int32)[:, None] - LAGS // 2
    angle = (bins * lagged % L).astype(jnp.float32) * (2.0 * math.pi / L)
    table = jnp.stack([jnp.cos(angle), -jnp.sin(angle)], axis=1).astype(jnp.bfloat16)
    return (smoother, taper, table)

def whiten_window(trace, smoother, taper):
    width = NB + 2 * HALF
    spec = jnp.fft.rfft(trace, axis=0)[F_LO - HALF:F_LO - HALF + width]
    real = jnp.real(spec).astype(jnp.float32)
    imag = jnp.imag(spec).astype(jnp.float32)
    power = real * real + imag * imag
    level = jnp.dot(smoother, power, precision=lax.Precision.HIGHEST) + 1e-06
    factor = taper[:, None] * lax.rsqrt(level)
    return jnp.stack([real[HALF:HALF + NB] * factor, imag[HALF:HALF + NB] * factor]).astype(jnp.bfloat16)

def reference(traces, pair_blocks):
    smoother, taper, table = band_tables()
    white = lax.map(lambda trace: whiten_window(trace, smoother, taper), traces)
    blocked = white.reshape(WINDOWS, 2, NB, BLOCKS, CH_DEV)
    table_wide = table.astype(jnp.float32)
    factor = 1.0 / math.sqrt(NB * WINDOWS)

    def one_slot(pair):
        left_block = jnp.maximum(pair[0], 0).astype(jnp.int32)
        right_block = jnp.maximum(pair[1], 0).astype(jnp.int32)
        left = lax.dynamic_index_in_dim(blocked, left_block, 3, keepdims=False).astype(jnp.float32)
        right = lax.dynamic_index_in_dim(blocked, right_block, 3, keepdims=False).astype(jnp.float32)
        real = left[:, 0] * right[:, 0] + left[:, 1] * right[:, 1]
        imag = left[:, 1] * right[:, 0] - left[:, 0] * right[:, 1]
        cross = jnp.stack([real, imag], axis=1).astype(jnp.bfloat16)
        cross = lax.optimization_barrier(cross)
        summed = lax.optimization_barrier(jnp.sum(cross.astype(jnp.float32), axis=0))
        corr = jnp.einsum('tqb,qbk->tk', table_wide, summed, precision=lax.Precision.HIGHEST) * factor
        return jnp.where(pair[0] >= 0, corr, jnp.zeros_like(corr))
    return lax.map(one_slot, pair_blocks)
```

```python
import math

import jax
import jax.numpy as jnp
from jax import lax
from jax.sharding import PartitionSpec as P

L = 15000
NB = 512
F_LO = 64
HALF = 32
LAGS = 512
REACH = 3

two_pi = 2.0 * math.pi


def band_tables():
    width = NB + 2 * HALF
    rows = lax.broadcasted_iota(jnp.int32, (NB, width), 0)
    cols = lax.broadcasted_iota(jnp.int32, (NB, width), 1)
    smoother = jnp.where(
        (cols >= rows) & (cols <= rows + 2 * HALF), 1.0 / (2 * HALF + 1), 0.0
    ).astype(jnp.float32)
    taper = jnp.sin(
        math.pi * (lax.broadcasted_iota(jnp.int32, (NB,), 0).astype(jnp.float32) + 0.5) / NB
    )
    bins = F_LO + lax.broadcasted_iota(jnp.int32, (LAGS, NB), 1)
    lagged = lax.broadcasted_iota(jnp.int32, (LAGS, NB), 0) - LAGS // 2
    angle = (bins * lagged % L).astype(jnp.float32) * (two_pi / L)
    table = jnp.stack([jnp.cos(angle), -jnp.sin(angle)], axis=1).astype(jnp.bfloat16)
    return (smoother, taper, table)


def band_dft(x, f0, nbins, outer=125, prec=lax.Precision.HIGH):
    total, channels = x.shape
    inner = total // outer
    half = outer // 2 + 1
    xb = x.reshape(outer, inner, channels)
    r = lax.broadcasted_iota(jnp.int32, (half, outer), 0)
    b = lax.broadcasted_iota(jnp.int32, (half, outer), 1)
    ang1 = ((r * b) % outer).astype(jnp.float32) * (two_pi / outer)
    basis1 = jnp.concatenate([jnp.cos(ang1), -jnp.sin(ang1)], axis=0)
    z = jnp.einsum("rb,bac->rac", basis1, xb, precision=prec, preferred_element_type=jnp.float32)
    zr, zi = z[:half], z[half:]
    r2 = lax.broadcasted_iota(jnp.int32, (half, inner), 0)
    a2 = lax.broadcasted_iota(jnp.int32, (half, inner), 1)
    ang2 = ((r2 * a2) % total).astype(jnp.float32) * (two_pi / total)
    dc = jnp.cos(ang2)[:, :, None]
    ds = jnp.sin(ang2)[:, :, None]
    wr = dc * zr + ds * zi
    wi = dc * zi - ds * zr
    nj = (f0 + nbins + outer - 1) // outer + 1
    j3 = lax.broadcasted_iota(jnp.int32, (nj, inner), 0)
    a3 = lax.broadcasted_iota(jnp.int32, (nj, inner), 1)
    ang3 = ((j3 * a3) % inner).astype(jnp.float32) * (two_pi / inner)
    basis2 = jnp.concatenate([jnp.cos(ang3), jnp.sin(ang3)], axis=0)
    u = jnp.einsum(
        "ja,srac->sjrc", basis2, jnp.stack([wr, wi]), precision=prec,
        preferred_element_type=jnp.float32,
    )
    u1, u4 = u[0, :nj], u[0, nj:]
    u3, u2 = u[1, :nj], u[1, nj:]
    dre, dim = u1 + u2, u3 - u4
    cre, cim = u1 - u2, -u3 - u4
    res_re, res_im = [], []
    f = f0
    end = f0 + nbins
    while f < end:
        j, rr = divmod(f, outer)
        if rr < half:
            stop = min(half, rr + (end - f))
            res_re.append(dre[j, rr:stop])
            res_im.append(dim[j, rr:stop])
            f += stop - rr
        else:
            s0 = outer * (j + 1) - f
            s_end = max(0, s0 - (end - f))
            res_re.append(jnp.flip(cre[j + 1, s_end + 1 : s0 + 1], axis=0))
            res_im.append(jnp.flip(cim[j + 1, s_end + 1 : s0 + 1], axis=0))
            f += s0 - s_end
    return jnp.concatenate(res_re, 0), jnp.concatenate(res_im, 0)


def whiten_local(trace, smoother, taper):
    width = NB + 2 * HALF
    real, imag = band_dft(trace, F_LO - HALF, width)
    power = real * real + imag * imag
    level = jnp.dot(smoother, power, precision=lax.Precision.HIGHEST) + 1e-06
    factor = taper[:, None] * lax.rsqrt(level)
    white = jnp.stack([real[HALF : HALF + NB] * factor, imag[HALF : HALF + NB] * factor])
    return white.astype(jnp.bfloat16)


def cross_spectra(left, right):
    left_re = left[..., 0, :, :].astype(jnp.float32)
    left_im = left[..., 1, :, :].astype(jnp.float32)
    right_re = right[..., 0, :, :].astype(jnp.float32)
    right_im = right[..., 1, :, :].astype(jnp.float32)
    real = left_re * right_re + left_im * right_im
    imag = left_im * right_re - left_re * right_im
    return jnp.stack([real, imag], axis=-3).astype(jnp.bfloat16)


def body(traces, pair_blocks):
    smoother, taper, table = band_tables()
    white = whiten_local(traces[0], smoother, taper)
    blocks = lax.axis_size("chan")
    windows_all = traces.shape[0] * lax.axis_size("win")
    factor = 1.0 / math.sqrt(NB * windows_all)
    partners = []
    for d in range(1, REACH + 1):
        perm = [(i + d, i) for i in range(blocks - d)]
        partners.append(lax.ppermute(white, "chan", perm))
    right = jnp.stack(partners)
    cross = cross_spectra(white[None], right)
    corr = jnp.einsum("tqb,dqbk->tdk", table, cross, preferred_element_type=jnp.float32) * factor
    corr = lax.psum_scatter(corr, "win", scatter_dimension=0, tiled=True)
    every = lax.all_gather(corr, "chan", axis=0)
    left_block = pair_blocks[:, 0]
    offset = pair_blocks[:, 1] - pair_blocks[:, 0]
    filled = left_block >= 0
    block_index = jnp.where(filled, left_block, 0)
    offset_index = jnp.where(filled, offset - 1, 0)
    picked = every[block_index, :, offset_index, :]
    return jnp.where(filled[:, None, None], picked, 0.0)


def solution(mesh):
    in_specs = (P("win", None, "chan"), P("chan", None))
    out_specs = P("chan", "win", None)
    return jax.shard_map(body, mesh=mesh, in_specs=in_specs, out_specs=out_specs, check_vma=False)
```

```python
import math

import jax
import jax.numpy as jnp
from jax import lax
from jax.sharding import PartitionSpec as P

L = 15000
NB = 512
F_LO = 64
HALF = 32
LAGS = 512
REACH = 3

two_pi = 2.0 * math.pi


def band_tables():
    width = NB + 2 * HALF
    rows = lax.broadcasted_iota(jnp.int32, (NB, width), 0)
    cols = lax.broadcasted_iota(jnp.int32, (NB, width), 1)
    smoother = jnp.where(
        (cols >= rows) & (cols <= rows + 2 * HALF), 1.0 / (2 * HALF + 1), 0.0
    ).astype(jnp.float32)
    taper = jnp.sin(
        math.pi * (lax.broadcasted_iota(jnp.int32, (NB,), 0).astype(jnp.float32) + 0.5) / NB
    )
    bins = F_LO + lax.broadcasted_iota(jnp.int32, (LAGS, NB), 1)
    lagged = lax.broadcasted_iota(jnp.int32, (LAGS, NB), 0) - LAGS // 2
    angle = (bins * lagged % L).astype(jnp.float32) * (two_pi / L)
    table = jnp.stack([jnp.cos(angle), -jnp.sin(angle)], axis=1).astype(jnp.bfloat16)
    return (smoother, taper, table)


def band_dft(x, f0, nbins, outer=125, prec=lax.Precision.HIGH):
    total, channels = x.shape
    inner = total // outer
    half = outer // 2 + 1
    xb = x.reshape(outer, inner, channels)
    r = lax.broadcasted_iota(jnp.int32, (half, outer), 0)
    b = lax.broadcasted_iota(jnp.int32, (half, outer), 1)
    ang1 = ((r * b) % outer).astype(jnp.float32) * (two_pi / outer)
    basis1 = jnp.concatenate([jnp.cos(ang1), -jnp.sin(ang1)], axis=0)
    z = jnp.einsum("rb,bac->rac", basis1, xb, precision=prec, preferred_element_type=jnp.float32)
    zr, zi = z[:half], z[half:]
    r2 = lax.broadcasted_iota(jnp.int32, (half, inner), 0)
    a2 = lax.broadcasted_iota(jnp.int32, (half, inner), 1)
    ang2 = ((r2 * a2) % total).astype(jnp.float32) * (two_pi / total)
    dc = jnp.cos(ang2)[:, :, None]
    ds = jnp.sin(ang2)[:, :, None]
    wr = dc * zr + ds * zi
    wi = dc * zi - ds * zr
    nj = (f0 + nbins + outer - 1) // outer + 1
    j3 = lax.broadcasted_iota(jnp.int32, (nj, inner), 0)
    a3 = lax.broadcasted_iota(jnp.int32, (nj, inner), 1)
    ang3 = ((j3 * a3) % inner).astype(jnp.float32) * (two_pi / inner)
    basis2 = jnp.concatenate([jnp.cos(ang3), jnp.sin(ang3)], axis=0)
    u = jnp.einsum(
        "ja,srac->sjrc", basis2, jnp.stack([wr, wi]), precision=prec,
        preferred_element_type=jnp.float32,
    )
    u1, u4 = u[0, :nj], u[0, nj:]
    u3, u2 = u[1, :nj], u[1, nj:]
    dre, dim = u1 + u2, u3 - u4
    cre, cim = u1 - u2, -u3 - u4
    res_re, res_im = [], []
    f = f0
    end = f0 + nbins
    while f < end:
        j, rr = divmod(f, outer)
        if rr < half:
            stop = min(half, rr + (end - f))
            res_re.append(dre[j, rr:stop])
            res_im.append(dim[j, rr:stop])
            f += stop - rr
        else:
            s0 = outer * (j + 1) - f
            s_end = max(0, s0 - (end - f))
            res_re.append(jnp.flip(cre[j + 1, s_end + 1 : s0 + 1], axis=0))
            res_im.append(jnp.flip(cim[j + 1, s_end + 1 : s0 + 1], axis=0))
            f += s0 - s_end
    return jnp.concatenate(res_re, 0), jnp.concatenate(res_im, 0)


def whiten_local(trace, smoother, taper):
    width = NB + 2 * HALF
    real, imag = band_dft(trace, F_LO - HALF, width)
    power = real * real + imag * imag
    level = jnp.dot(smoother, power, precision=lax.Precision.HIGHEST) + 1e-06
    factor = taper[:, None] * lax.rsqrt(level)
    white = jnp.stack([real[HALF : HALF + NB] * factor, imag[HALF : HALF + NB] * factor])
    return white.astype(jnp.bfloat16)


def cross_spectra(left, right):
    left_re = left[..., 0, :, :].astype(jnp.float32)
    left_im = left[..., 1, :, :].astype(jnp.float32)
    right_re = right[..., 0, :, :].astype(jnp.float32)
    right_im = right[..., 1, :, :].astype(jnp.float32)
    real = left_re * right_re + left_im * right_im
    imag = left_im * right_re - left_re * right_im
    return jnp.stack([real, imag], axis=-3).astype(jnp.bfloat16)


def body(traces, pair_blocks):
    smoother, taper, table = band_tables()
    white = whiten_local(traces[0], smoother, taper)
    nx = lax.axis_size("cx")
    nz = lax.axis_size("cz")
    blocks = nx * nz
    nwin = lax.axis_size("win")
    windows_all = traces.shape[0] * nwin
    factor = 1.0 / math.sqrt(NB * windows_all)
    received = {}
    for shift in (-1, 1, 2):
        perm = [(k + shift, k) for k in range(blocks) if 0 <= k + shift < blocks]
        received[shift] = lax.ppermute(white, ("cx", "cz"), perm)
    left = jnp.stack([white, received[-1], received[-1]])
    right = jnp.stack([received[1], received[1], received[2]])
    cross = cross_spectra(left, right)
    corr = jnp.einsum("tqb,dqbk->tdk", table, cross, preferred_element_type=jnp.float32) * factor
    lags = corr.shape[0] // nwin
    corr = corr.reshape((nwin, lags) + corr.shape[1:])
    corr = lax.all_to_all(corr, "win", 0, 0).sum(axis=0)
    ring = lax.all_to_all(jnp.broadcast_to(corr[None], (nz,) + corr.shape), "cz", 0, 0)
    owners = lax.all_gather(pair_blocks, "cx", axis=0)
    lb = owners[..., 0]
    offset = owners[..., 1] - lb
    filled = lb >= 0
    holder = jnp.where(filled, lb + (offset > 1).astype(jnp.int32), 0)
    mine = filled & (holder // nz == lax.axis_index("cx"))
    zi = jnp.where(mine, holder % nz, 0)
    di = jnp.where(mine, offset - 1, 0)
    picked = ring[zi, :, di, :]
    picked = jnp.where(mine[..., None, None], picked, 0.0)
    got = lax.all_to_all(picked, "cx", 0, 0).sum(axis=0)
    return jnp.where(filled_local(pair_blocks)[:, None, None], got, 0.0)


def filled_local(pair_blocks):
    return pair_blocks[:, 0] >= 0


def solution(mesh):
    nx = 4
    devices = mesh.devices.reshape(mesh.devices.shape[0], nx, -1)
    grid = jax.sharding.Mesh(devices, ("win", "cx", "cz"))
    in_specs = (P("win", None, ("cx", "cz")), P(("cx", "cz"), None))
    out_specs = P(("cx", "cz"), "win", None)
    return jax.shard_map(body, mesh=grid, in_specs=in_specs, out_specs=out_specs, check_vma=False)
```

```python
import math

import jax
import ml_dtypes
import numpy as np
import jax.numpy as jnp
from jax import lax
from jax.sharding import PartitionSpec as P

L = 15000
NB = 512
F_LO = 64
HALF = 32
LAGS = 512
REACH = 3

two_pi = 2.0 * math.pi


def lag_table():
    bins = F_LO + np.arange(NB, dtype=np.int64)[None, :]
    lagged = np.arange(LAGS, dtype=np.int64)[:, None] - LAGS // 2
    angle = ((bins * lagged) % L).astype(np.float32) * np.float32(two_pi / L)
    angle = angle.astype(np.float64)
    table = np.stack([np.cos(angle), -np.sin(angle)], axis=1).astype(np.float32)
    return table.astype(ml_dtypes.bfloat16)


def band_tables():
    width = NB + 2 * HALF
    rows = lax.broadcasted_iota(jnp.int32, (NB, width), 0)
    cols = lax.broadcasted_iota(jnp.int32, (NB, width), 1)
    smoother = jnp.where(
        (cols >= rows) & (cols <= rows + 2 * HALF), 1.0 / (2 * HALF + 1), 0.0
    ).astype(jnp.float32)
    taper = jnp.sin(
        math.pi * (lax.broadcasted_iota(jnp.int32, (NB,), 0).astype(jnp.float32) + 0.5) / NB
    )
    table = jnp.asarray(lag_table())
    return (smoother, taper, table)


def band_dft(x, f0, nbins, outer=125, prec=lax.Precision.HIGH):
    total, channels = x.shape
    inner = total // outer
    half = outer // 2 + 1
    xb = x.reshape(outer, inner, channels)
    r = lax.broadcasted_iota(jnp.int32, (half, outer), 0)
    b = lax.broadcasted_iota(jnp.int32, (half, outer), 1)
    ang1 = ((r * b) % outer).astype(jnp.float32) * (two_pi / outer)
    basis1 = jnp.concatenate([jnp.cos(ang1), -jnp.sin(ang1)], axis=0)
    z = jnp.einsum("rb,bac->rac", basis1, xb, precision=prec, preferred_element_type=jnp.float32)
    zr, zi = z[:half], z[half:]
    r2 = lax.broadcasted_iota(jnp.int32, (half, inner), 0)
    a2 = lax.broadcasted_iota(jnp.int32, (half, inner), 1)
    ang2 = ((r2 * a2) % total).astype(jnp.float32) * (two_pi / total)
    dc = jnp.cos(ang2)[:, :, None]
    ds = jnp.sin(ang2)[:, :, None]
    wr = dc * zr + ds * zi
    wi = dc * zi - ds * zr
    nj = (f0 + nbins + outer - 1) // outer + 1
    j3 = lax.broadcasted_iota(jnp.int32, (nj, inner), 0)
    a3 = lax.broadcasted_iota(jnp.int32, (nj, inner), 1)
    ang3 = ((j3 * a3) % inner).astype(jnp.float32) * (two_pi / inner)
    basis2 = jnp.concatenate([jnp.cos(ang3), jnp.sin(ang3)], axis=0)
    u = jnp.einsum(
        "ja,srac->sjrc", basis2, jnp.stack([wr, wi]), precision=prec,
        preferred_element_type=jnp.float32,
    )
    u1, u4 = u[0, :nj], u[0, nj:]
    u3, u2 = u[1, :nj], u[1, nj:]
    dre, dim = u1 + u2, u3 - u4
    cre, cim = u1 - u2, -u3 - u4
    res_re, res_im = [], []
    f = f0
    end = f0 + nbins
    while f < end:
        j, rr = divmod(f, outer)
        if rr < half:
            stop = min(half, rr + (end - f))
            res_re.append(dre[j, rr:stop])
            res_im.append(dim[j, rr:stop])
            f += stop - rr
        else:
            s0 = outer * (j + 1) - f
            s_end = max(0, s0 - (end - f))
            res_re.append(jnp.flip(cre[j + 1, s_end + 1 : s0 + 1], axis=0))
            res_im.append(jnp.flip(cim[j + 1, s_end + 1 : s0 + 1], axis=0))
            f += s0 - s_end
    return jnp.concatenate(res_re, 0), jnp.concatenate(res_im, 0)


def whiten_local(trace, smoother, taper):
    width = NB + 2 * HALF
    real, imag = band_dft(trace, F_LO - HALF, width)
    power = real * real + imag * imag
    level = jnp.dot(smoother, power, precision=lax.Precision.HIGHEST) + 1e-06
    factor = taper[:, None] * lax.rsqrt(level)
    white = jnp.stack([real[HALF : HALF + NB] * factor, imag[HALF : HALF + NB] * factor])
    return white.astype(jnp.bfloat16)


def cross_spectra(left, right):
    left_re = left[..., 0, :, :].astype(jnp.float32)
    left_im = left[..., 1, :, :].astype(jnp.float32)
    right_re = right[..., 0, :, :].astype(jnp.float32)
    right_im = right[..., 1, :, :].astype(jnp.float32)
    real = left_re * right_re + left_im * right_im
    imag = left_im * right_re - left_re * right_im
    return jnp.stack([real, imag], axis=-3).astype(jnp.bfloat16)


def body(traces, pair_blocks):
    smoother, taper, table = band_tables()
    white = whiten_local(traces[0], smoother, taper)
    nx = lax.axis_size("cx")
    nz = lax.axis_size("cz")
    blocks = nx * nz
    nwin = lax.axis_size("win")
    windows_all = traces.shape[0] * nwin
    factor = 1.0 / math.sqrt(NB * windows_all)
    received = {}
    for shift in (-1, 2):
        perm = [(k + shift, k) for k in range(blocks) if 0 <= k + shift < blocks]
        received[shift] = lax.ppermute(white, ("cx", "cz"), perm)
    left = jnp.stack([received[-1], white, received[-1]])
    right = jnp.stack([white, received[2], received[2]])
    cross = cross_spectra(left, right)
    corr = jnp.einsum("tqb,dqbk->tdk", table, cross, preferred_element_type=jnp.float32) * factor
    lags = corr.shape[0] // nwin
    corr = corr.reshape((nwin, lags) + corr.shape[1:])
    corr = lax.all_to_all(corr, "win", 0, 0).sum(axis=0)
    ring = lax.all_to_all(jnp.broadcast_to(corr[None], (nz,) + corr.shape), "cz", 0, 0)
    me_x = lax.axis_index("cx")
    shifted = [pair_blocks]
    for step in range(1, nx):
        shifted.append(lax.ppermute(pair_blocks, "cx", [(k, (k + step) % nx) for k in range(nx)]))
    shifted = jnp.stack(shifted)
    owners = shifted[(me_x - jnp.arange(nx)) % nx]
    lb = owners[..., 0]
    offset = owners[..., 1] - lb
    filled = lb >= 0
    holder = jnp.where(filled, lb + (offset != 2).astype(jnp.int32), 0)
    mine = filled & (holder // nz == me_x)
    zi = jnp.where(mine, holder % nz, 0)
    di = jnp.where(mine, offset - 1, 0)
    picked = ring[zi, :, di, :]
    picked = jnp.where(mine[..., None, None], picked, 0.0)
    got = lax.all_to_all(picked, "cx", 0, 0).sum(axis=0)
    return jnp.where(filled_local(pair_blocks)[:, None, None], got, 0.0)


def filled_local(pair_blocks):
    return pair_blocks[:, 0] >= 0


def solution(mesh):
    nx = 4
    devices = mesh.devices.reshape(mesh.devices.shape[0], nx, -1)
    grid = jax.sharding.Mesh(devices, ("win", "cx", "cz"))
    in_specs = (P("win", None, ("cx", "cz")), P(("cx", "cz"), None))
    out_specs = P(("cx", "cz"), "win", None)
    return jax.shard_map(body, mesh=grid, in_specs=in_specs, out_specs=out_specs, check_vma=False)
```

```python
import math

import jax
import jax.numpy as jnp
from jax import lax
from jax.sharding import PartitionSpec as P

L = 15000
NB = 512
F_LO = 64
HALF = 32
LAGS = 512
REACH = 3

two_pi = 2.0 * math.pi


def band_tables():
    width = NB + 2 * HALF
    rows = lax.broadcasted_iota(jnp.int32, (NB, width), 0)
    cols = lax.broadcasted_iota(jnp.int32, (NB, width), 1)
    smoother = jnp.where(
        (cols >= rows) & (cols <= rows + 2 * HALF), 1.0 / (2 * HALF + 1), 0.0
    ).astype(jnp.float32)
    taper = jnp.sin(
        math.pi * (lax.broadcasted_iota(jnp.int32, (NB,), 0).astype(jnp.float32) + 0.5) / NB
    )
    bins = F_LO + lax.broadcasted_iota(jnp.int32, (LAGS, NB), 1)
    lagged = lax.broadcasted_iota(jnp.int32, (LAGS, NB), 0) - LAGS // 2
    angle = (bins * lagged % L).astype(jnp.float32) * (two_pi / L)
    table = jnp.stack([jnp.cos(angle), -jnp.sin(angle)], axis=1).astype(jnp.bfloat16)
    return (smoother, taper, table)


def band_dft(x, f0, nbins, outer=125, prec=lax.Precision.HIGH):
    total, channels = x.shape
    inner = total // outer
    half = outer // 2 + 1
    xb = x.reshape(outer, inner, channels)
    r = lax.broadcasted_iota(jnp.int32, (half, outer), 0)
    b = lax.broadcasted_iota(jnp.int32, (half, outer), 1)
    ang1 = ((r * b) % outer).astype(jnp.float32) * (two_pi / outer)
    basis1 = jnp.concatenate([jnp.cos(ang1), -jnp.sin(ang1)], axis=0)
    z = jnp.einsum("rb,bac->rac", basis1, xb, precision=prec, preferred_element_type=jnp.float32)
    zr, zi = z[:half], z[half:]
    r2 = lax.broadcasted_iota(jnp.int32, (half, inner), 0)
    a2 = lax.broadcasted_iota(jnp.int32, (half, inner), 1)
    ang2 = ((r2 * a2) % total).astype(jnp.float32) * (two_pi / total)
    dc = jnp.cos(ang2)[:, :, None]
    ds = jnp.sin(ang2)[:, :, None]
    wr = dc * zr + ds * zi
    wi = dc * zi - ds * zr
    nj = (f0 + nbins + outer - 1) // outer + 1
    j3 = lax.broadcasted_iota(jnp.int32, (nj, inner), 0)
    a3 = lax.broadcasted_iota(jnp.int32, (nj, inner), 1)
    ang3 = ((j3 * a3) % inner).astype(jnp.float32) * (two_pi / inner)
    basis2 = jnp.concatenate([jnp.cos(ang3), jnp.sin(ang3)], axis=0)
    u = jnp.einsum(
        "ja,srac->sjrc", basis2, jnp.stack([wr, wi]), precision=prec,
        preferred_element_type=jnp.float32,
    )
    u1, u4 = u[0, :nj], u[0, nj:]
    u3, u2 = u[1, :nj], u[1, nj:]
    dre, dim = u1 + u2, u3 - u4
    cre, cim = u1 - u2, -u3 - u4
    res_re, res_im = [], []
    f = f0
    end = f0 + nbins
    while f < end:
        j, rr = divmod(f, outer)
        if rr < half:
            stop = min(half, rr + (end - f))
            res_re.append(dre[j, rr:stop])
            res_im.append(dim[j, rr:stop])
            f += stop - rr
        else:
            s0 = outer * (j + 1) - f
            s_end = max(0, s0 - (end - f))
            res_re.append(jnp.flip(cre[j + 1, s_end + 1 : s0 + 1], axis=0))
            res_im.append(jnp.flip(cim[j + 1, s_end + 1 : s0 + 1], axis=0))
            f += s0 - s_end
    return jnp.concatenate(res_re, 0), jnp.concatenate(res_im, 0)


def whiten_local(trace, smoother, taper):
    width = NB + 2 * HALF
    real, imag = band_dft(trace, F_LO - HALF, width)
    power = real * real + imag * imag
    level = jnp.dot(smoother, power, precision=lax.Precision.HIGHEST) + 1e-06
    factor = taper[:, None] * lax.rsqrt(level)
    white = jnp.stack([real[HALF : HALF + NB] * factor, imag[HALF : HALF + NB] * factor])
    return white.astype(jnp.bfloat16)


def cross_spectra(left, right):
    left_re = left[..., 0, :, :].astype(jnp.float32)
    left_im = left[..., 1, :, :].astype(jnp.float32)
    right_re = right[..., 0, :, :].astype(jnp.float32)
    right_im = right[..., 1, :, :].astype(jnp.float32)
    real = left_re * right_re + left_im * right_im
    imag = left_im * right_re - left_re * right_im
    return jnp.stack([real, imag], axis=-3).astype(jnp.bfloat16)


def body(traces, pair_blocks):
    smoother, taper, table = band_tables()
    white = whiten_local(traces[0], smoother, taper)
    nx = lax.axis_size("cx")
    nz = lax.axis_size("cz")
    blocks = nx * nz
    nwin = lax.axis_size("win")
    windows_all = traces.shape[0] * nwin
    factor = 1.0 / math.sqrt(NB * windows_all)
    received = {}
    for shift in (-1, 2):
        perm = [(k + shift, k) for k in range(blocks) if 0 <= k + shift < blocks]
        received[shift] = lax.ppermute(white, ("cx", "cz"), perm)
    left = jnp.stack([received[-1], white, received[-1]])
    right = jnp.stack([white, received[2], received[2]])
    cross = cross_spectra(left, right)
    corr = jnp.einsum("tqb,dqbk->tdk", table, cross, preferred_element_type=jnp.float32) * factor
    lags = corr.shape[0] // nwin
    corr = corr.reshape((nwin, lags) + corr.shape[1:])
    corr = lax.all_to_all(corr, "win", 0, 0).sum(axis=0)
    forward, backward = corr, corr
    gathered = {0: corr}
    for step in range(1, nz // 2 + 1):
        forward = lax.ppermute(forward, "cz", [(k, (k + 1) % nz) for k in range(nz)])
        gathered[-step % nz] = forward
        if step < nz - nz // 2:
            backward = lax.ppermute(backward, "cz", [(k, (k - 1) % nz) for k in range(nz)])
            gathered[step % nz] = backward
    ring = jnp.stack([gathered[j] for j in range(nz)])
    me_x = lax.axis_index("cx")
    shifted = [pair_blocks]
    for step in range(1, nx):
        shifted.append(lax.ppermute(pair_blocks, "cx", [(k, (k + step) % nx) for k in range(nx)]))
    shifted = jnp.stack(shifted)
    owners = shifted[(me_x - jnp.arange(nx)) % nx]
    lb = owners[..., 0]
    offset = owners[..., 1] - lb
    filled = lb >= 0
    holder = jnp.where(filled, lb + (offset != 2).astype(jnp.int32), 0)
    mine = filled & (holder // nz == me_x)
    zi = jnp.where(mine, (holder - lax.axis_index("cz")) % nz, 0)
    di = jnp.where(mine, offset - 1, 0)
    picked = ring[zi, :, di, :]
    picked = jnp.where(mine[..., None, None], picked, 0.0)
    got = lax.dynamic_index_in_dim(picked, me_x, 0, keepdims=False)
    for step in range(1, nx):
        chunk = lax.dynamic_index_in_dim(picked, (me_x + step) % nx, 0, keepdims=False)
        got = got + lax.ppermute(chunk, "cx", [(k, (k + step) % nx) for k in range(nx)])
    return jnp.where(filled_local(pair_blocks)[:, None, None], got, 0.0)


def filled_local(pair_blocks):
    return pair_blocks[:, 0] >= 0


def solution(mesh):
    nx = 4
    devices = mesh.devices.reshape(mesh.devices.shape[0], nx, -1)
    grid = jax.sharding.Mesh(devices, ("win", "cx", "cz"))
    in_specs = (P("win", None, ("cx", "cz")), P(("cx", "cz"), None))
    out_specs = P(("cx", "cz"), "win", None)
    return jax.shard_map(body, mesh=grid, in_specs=in_specs, out_specs=out_specs, check_vma=False)
```

```python
import math

import jax
import jax.numpy as jnp
from jax import lax
from jax.sharding import PartitionSpec as P

L = 15000
NB = 512
F_LO = 64
HALF = 32
LAGS = 512
REACH = 3

two_pi = 2.0 * math.pi


def band_tables():
    width = NB + 2 * HALF
    rows = lax.broadcasted_iota(jnp.int32, (NB, width), 0)
    cols = lax.broadcasted_iota(jnp.int32, (NB, width), 1)
    smoother = jnp.where(
        (cols >= rows) & (cols <= rows + 2 * HALF), 1.0 / (2 * HALF + 1), 0.0
    ).astype(jnp.float32)
    taper = jnp.sin(
        math.pi * (lax.broadcasted_iota(jnp.int32, (NB,), 0).astype(jnp.float32) + 0.5) / NB
    )
    bins = F_LO + lax.broadcasted_iota(jnp.int32, (LAGS, NB), 1)
    lagged = lax.broadcasted_iota(jnp.int32, (LAGS, NB), 0) - LAGS // 2
    angle = (bins * lagged % L).astype(jnp.float32) * (two_pi / L)
    table = jnp.stack([jnp.cos(angle), -jnp.sin(angle)], axis=1).astype(jnp.bfloat16)
    return (smoother, taper, table)


def band_dft(x, f0, nbins, outer=125, prec=lax.Precision.HIGH):
    total, channels = x.shape
    inner = total // outer
    half = outer // 2 + 1
    xb = x.reshape(outer, inner, channels)
    r = lax.broadcasted_iota(jnp.int32, (half, outer), 0)
    b = lax.broadcasted_iota(jnp.int32, (half, outer), 1)
    ang1 = ((r * b) % outer).astype(jnp.float32) * (two_pi / outer)
    basis1 = jnp.concatenate([jnp.cos(ang1), -jnp.sin(ang1)], axis=0)
    z = jnp.einsum("rb,bac->rac", basis1, xb, precision=prec, preferred_element_type=jnp.float32)
    zr, zi = z[:half], z[half:]
    r2 = lax.broadcasted_iota(jnp.int32, (half, inner), 0)
    a2 = lax.broadcasted_iota(jnp.int32, (half, inner), 1)
    ang2 = ((r2 * a2) % total).astype(jnp.float32) * (two_pi / total)
    dc = jnp.cos(ang2)[:, :, None]
    ds = jnp.sin(ang2)[:, :, None]
    wr = dc * zr + ds * zi
    wi = dc * zi - ds * zr
    nj = (f0 + nbins + outer - 1) // outer + 1
    j3 = lax.broadcasted_iota(jnp.int32, (nj, inner), 0)
    a3 = lax.broadcasted_iota(jnp.int32, (nj, inner), 1)
    ang3 = ((j3 * a3) % inner).astype(jnp.float32) * (two_pi / inner)
    basis2 = jnp.concatenate([jnp.cos(ang3), jnp.sin(ang3)], axis=0)
    u = jnp.einsum(
        "ja,srac->sjrc", basis2, jnp.stack([wr, wi]), precision=prec,
        preferred_element_type=jnp.float32,
    )
    u1, u4 = u[0, :nj], u[0, nj:]
    u3, u2 = u[1, :nj], u[1, nj:]
    dre, dim = u1 + u2, u3 - u4
    cre, cim = u1 - u2, -u3 - u4
    res_re, res_im = [], []
    f = f0
    end = f0 + nbins
    while f < end:
        j, rr = divmod(f, outer)
        if rr < half:
            stop = min(half, rr + (end - f))
            res_re.append(dre[j, rr:stop])
            res_im.append(dim[j, rr:stop])
            f += stop - rr
        else:
            s0 = outer * (j + 1) - f
            s_end = max(0, s0 - (end - f))
            res_re.append(jnp.flip(cre[j + 1, s_end + 1 : s0 + 1], axis=0))
            res_im.append(jnp.flip(cim[j + 1, s_end + 1 : s0 + 1], axis=0))
            f += s0 - s_end
    return jnp.concatenate(res_re, 0), jnp.concatenate(res_im, 0)


def whiten_local(trace, smoother, taper):
    width = NB + 2 * HALF
    real, imag = band_dft(trace, F_LO - HALF, width)
    power = real * real + imag * imag
    level = jnp.dot(smoother, power, precision=lax.Precision.HIGHEST) + 1e-06
    factor = taper[:, None] * lax.rsqrt(level)
    white = jnp.stack([real[HALF : HALF + NB] * factor, imag[HALF : HALF + NB] * factor])
    return white.astype(jnp.bfloat16)


def cross_spectra(left, right):
    left_re = left[..., 0, :, :].astype(jnp.float32)
    left_im = left[..., 1, :, :].astype(jnp.float32)
    right_re = right[..., 0, :, :].astype(jnp.float32)
    right_im = right[..., 1, :, :].astype(jnp.float32)
    real = left_re * right_re + left_im * right_im
    imag = left_im * right_re - left_re * right_im
    return jnp.stack([real, imag], axis=-3).astype(jnp.bfloat16)


def body(traces, pair_blocks):
    smoother, taper, table = band_tables()
    white = whiten_local(traces[0], smoother, taper)
    nx = lax.axis_size("cx")
    nz = lax.axis_size("cz")
    blocks = nx * nz
    nwin = lax.axis_size("win")
    windows_all = traces.shape[0] * nwin
    factor = 1.0 / math.sqrt(NB * windows_all)
    received = {}
    for shift in (-1, 2):
        perm = [(k + shift, k) for k in range(blocks) if 0 <= k + shift < blocks]
        received[shift] = lax.ppermute(white, ("cx", "cz"), perm)
    left = jnp.stack([received[-1], white, received[-1]])
    right = jnp.stack([white, received[2], received[2]])
    cross = cross_spectra(left, right)
    corr = jnp.einsum("tqb,dqbk->tdk", table, cross, preferred_element_type=jnp.float32) * factor
    lags = corr.shape[0] // nwin
    corr = corr.reshape((nwin, lags) + corr.shape[1:])
    corr = lax.all_to_all(corr, "win", 0, 0).sum(axis=0)
    def shift_z(value, step):
        return lax.ppermute(value, "cz", [(k, (k - step) % nz) for k in range(nz)])

    gathered = {0: corr}
    for step in (1, -1, 2, -2):
        gathered[step % nz] = shift_z(corr, step)
    ahead = shift_z(jnp.stack([gathered[1], gathered[2]]), 2)
    behind = shift_z(gathered[nz - 1], -2)
    gathered[3], gathered[4] = ahead[0], ahead[1]
    gathered[nz - 3] = behind
    ring = jnp.stack([gathered[j] for j in range(nz)])
    me_x = lax.axis_index("cx")
    shifted = [pair_blocks]
    for step in range(1, nx):
        shifted.append(lax.ppermute(pair_blocks, "cx", [(k, (k + step) % nx) for k in range(nx)]))
    shifted = jnp.stack(shifted)
    owners = shifted[(me_x - jnp.arange(nx)) % nx]
    lb = owners[..., 0]
    offset = owners[..., 1] - lb
    filled = lb >= 0
    holder = jnp.where(filled, lb + (offset != 2).astype(jnp.int32), 0)
    mine = filled & (holder // nz == me_x)
    zi = jnp.where(mine, (holder - lax.axis_index("cz")) % nz, 0)
    di = jnp.where(mine, offset - 1, 0)
    picked = ring[zi, :, di, :]
    picked = jnp.where(mine[..., None, None], picked, 0.0)
    got = lax.dynamic_index_in_dim(picked, me_x, 0, keepdims=False)
    for step in range(1, nx):
        chunk = lax.dynamic_index_in_dim(picked, (me_x + step) % nx, 0, keepdims=False)
        got = got + lax.ppermute(chunk, "cx", [(k, (k + step) % nx) for k in range(nx)])
    return jnp.where(filled_local(pair_blocks)[:, None, None], got, 0.0)


def filled_local(pair_blocks):
    return pair_blocks[:, 0] >= 0


def solution(mesh):
    nx = 4
    devices = mesh.devices.reshape(mesh.devices.shape[0], nx, -1)
    grid = jax.sharding.Mesh(devices, ("win", "cx", "cz"))
    in_specs = (P("win", None, ("cx", "cz")), P(("cx", "cz"), None))
    out_specs = P(("cx", "cz"), "win", None)
    return jax.shard_map(body, mesh=grid, in_specs=in_specs, out_specs=out_specs, check_vma=False)
```

```python
import math

import jax
import jax.numpy as jnp
from jax import lax
from jax.sharding import PartitionSpec as P

L = 15000
NB = 512
F_LO = 64
HALF = 32
LAGS = 512
REACH = 3

two_pi = 2.0 * math.pi


def band_tables():
    width = NB + 2 * HALF
    rows = lax.broadcasted_iota(jnp.int32, (NB, width), 0)
    cols = lax.broadcasted_iota(jnp.int32, (NB, width), 1)
    smoother = jnp.where(
        (cols >= rows) & (cols <= rows + 2 * HALF), 1.0 / (2 * HALF + 1), 0.0
    ).astype(jnp.float32)
    taper = jnp.sin(
        math.pi * (lax.broadcasted_iota(jnp.int32, (NB,), 0).astype(jnp.float32) + 0.5) / NB
    )
    bins = F_LO + lax.broadcasted_iota(jnp.int32, (LAGS, NB), 1)
    lagged = lax.broadcasted_iota(jnp.int32, (LAGS, NB), 0) - LAGS // 2
    angle = (bins * lagged % L).astype(jnp.float32) * (two_pi / L)
    table = jnp.stack([jnp.cos(angle), -jnp.sin(angle)], axis=1).astype(jnp.bfloat16)
    return (smoother, taper, table)


def band_dft(x, f0, nbins, tie, outer=125, prec=lax.Precision.HIGH):
    total, channels = x.shape
    inner = total // outer
    half = outer // 2 + 1
    xb = x.reshape(outer, inner, channels)
    r = lax.broadcasted_iota(jnp.int32, (half, outer), 0)
    b = lax.broadcasted_iota(jnp.int32, (half, outer), 1)
    ang1 = ((r * b) % outer).astype(jnp.float32) * (two_pi / outer)
    basis1 = jnp.concatenate([jnp.cos(ang1), -jnp.sin(ang1)], axis=0)
    z = jnp.einsum("rb,bac->rac", basis1, xb, precision=prec, preferred_element_type=jnp.float32)
    z, tie = lax.optimization_barrier((z, tie))
    zr, zi = z[:half], z[half:]
    r2 = lax.broadcasted_iota(jnp.int32, (half, inner), 0)
    a2 = lax.broadcasted_iota(jnp.int32, (half, inner), 1)
    ang2 = ((r2 * a2) % total).astype(jnp.float32) * (two_pi / total)
    dc = jnp.cos(ang2)[:, :, None]
    ds = jnp.sin(ang2)[:, :, None]
    wr = dc * zr + ds * zi
    wi = dc * zi - ds * zr
    nj = (f0 + nbins + outer - 1) // outer + 1
    j3 = lax.broadcasted_iota(jnp.int32, (nj, inner), 0)
    a3 = lax.broadcasted_iota(jnp.int32, (nj, inner), 1)
    ang3 = ((j3 * a3) % inner).astype(jnp.float32) * (two_pi / inner)
    basis2 = jnp.concatenate([jnp.cos(ang3), jnp.sin(ang3)], axis=0)
    u = jnp.einsum(
        "ja,srac->sjrc", basis2, jnp.stack([wr, wi]), precision=prec,
        preferred_element_type=jnp.float32,
    )
    u1, u4 = u[0, :nj], u[0, nj:]
    u3, u2 = u[1, :nj], u[1, nj:]
    dre, dim = u1 + u2, u3 - u4
    cre, cim = u1 - u2, -u3 - u4
    res_re, res_im = [], []
    f = f0
    end = f0 + nbins
    while f < end:
        j, rr = divmod(f, outer)
        if rr < half:
            stop = min(half, rr + (end - f))
            res_re.append(dre[j, rr:stop])
            res_im.append(dim[j, rr:stop])
            f += stop - rr
        else:
            s0 = outer * (j + 1) - f
            s_end = max(0, s0 - (end - f))
            res_re.append(jnp.flip(cre[j + 1, s_end + 1 : s0 + 1], axis=0))
            res_im.append(jnp.flip(cim[j + 1, s_end + 1 : s0 + 1], axis=0))
            f += s0 - s_end
    return jnp.concatenate(res_re, 0), jnp.concatenate(res_im, 0), tie


def whiten_local(trace, smoother, taper, tie):
    width = NB + 2 * HALF
    real, imag, tie = band_dft(trace, F_LO - HALF, width, tie)
    power = real * real + imag * imag
    level = jnp.dot(smoother, power, precision=lax.Precision.HIGHEST) + 1e-06
    factor = taper[:, None] * lax.rsqrt(level)
    white = jnp.stack([real[HALF : HALF + NB] * factor, imag[HALF : HALF + NB] * factor])
    return white.astype(jnp.bfloat16), tie


def cross_spectra(left, right):
    left_re = left[..., 0, :, :].astype(jnp.float32)
    left_im = left[..., 1, :, :].astype(jnp.float32)
    right_re = right[..., 0, :, :].astype(jnp.float32)
    right_im = right[..., 1, :, :].astype(jnp.float32)
    real = left_re * right_re + left_im * right_im
    imag = left_im * right_re - left_re * right_im
    return jnp.stack([real, imag], axis=-3).astype(jnp.bfloat16)


def body(traces, pair_blocks):
    smoother, taper, table = band_tables()
    nx = lax.axis_size("cx")
    me_x = lax.axis_index("cx")
    shifted = [pair_blocks]
    for step in range(1, nx):
        shifted.append(lax.ppermute(pair_blocks, "cx", [(k, (k + step) % nx) for k in range(nx)]))
    white, shifted = whiten_local(traces[0], smoother, taper, jnp.stack(shifted))
    nz = lax.axis_size("cz")
    blocks = nx * nz
    nwin = lax.axis_size("win")
    windows_all = traces.shape[0] * nwin
    factor = 1.0 / math.sqrt(NB * windows_all)
    received = {}
    for shift in (-1, 2):
        perm = [(k + shift, k) for k in range(blocks) if 0 <= k + shift < blocks]
        received[shift] = lax.ppermute(white, ("cx", "cz"), perm)
    left = jnp.stack([received[-1], white, received[-1]])
    right = jnp.stack([white, received[2], received[2]])
    cross = cross_spectra(left, right)
    corr = jnp.einsum("tqb,dqbk->tdk", table, cross, preferred_element_type=jnp.float32) * factor
    lags = corr.shape[0] // nwin
    corr = corr.reshape((nwin, lags) + corr.shape[1:])
    corr = lax.all_to_all(corr, "win", 0, 0).sum(axis=0)
    def shift_z(value, step):
        return lax.ppermute(value, "cz", [(k, (k - step) % nz) for k in range(nz)])

    gathered = {0: corr}
    for step in (1, -1, 2, -2):
        gathered[step % nz] = shift_z(corr, step)
    ahead = shift_z(jnp.stack([gathered[1], gathered[2]]), 2)
    behind = shift_z(gathered[nz - 1], -2)
    gathered[3], gathered[4] = ahead[0], ahead[1]
    gathered[nz - 3] = behind
    ring = jnp.stack([gathered[j] for j in range(nz)])
    owners = shifted[(me_x - jnp.arange(nx)) % nx]
    lb = owners[..., 0]
    offset = owners[..., 1] - lb
    filled = lb >= 0
    holder = jnp.where(filled, lb + (offset != 2).astype(jnp.int32), 0)
    mine = filled & (holder // nz == me_x)
    zi = jnp.where(mine, (holder - lax.axis_index("cz")) % nz, 0)
    di = jnp.where(mine, offset - 1, 0)
    picked = ring[zi, :, di, :]
    picked = jnp.where(mine[..., None, None], picked, 0.0)
    got = lax.dynamic_index_in_dim(picked, me_x, 0, keepdims=False)
    for step in range(1, nx):
        chunk = lax.dynamic_index_in_dim(picked, (me_x + step) % nx, 0, keepdims=False)
        got = got + lax.ppermute(chunk, "cx", [(k, (k + step) % nx) for k in range(nx)])
    return jnp.where(filled_local(pair_blocks)[:, None, None], got, 0.0)


def filled_local(pair_blocks):
    return pair_blocks[:, 0] >= 0


def solution(mesh):
    nx = 4
    devices = mesh.devices.reshape(mesh.devices.shape[0], nx, -1)
    grid = jax.sharding.Mesh(devices, ("win", "cx", "cz"))
    in_specs = (P("win", None, ("cx", "cz")), P(("cx", "cz"), None))
    out_specs = P(("cx", "cz"), "win", None)
    return jax.shard_map(body, mesh=grid, in_specs=in_specs, out_specs=out_specs, check_vma=False)
```

```python
import math

import jax
import jax.numpy as jnp
from jax import lax
from jax.sharding import PartitionSpec as P

L = 15000
NB = 512
F_LO = 64
HALF = 32
LAGS = 512
REACH = 3

two_pi = 2.0 * math.pi


def band_tables():
    width = NB + 2 * HALF
    rows = lax.broadcasted_iota(jnp.int32, (NB, width), 0)
    cols = lax.broadcasted_iota(jnp.int32, (NB, width), 1)
    smoother = jnp.where(
        (cols >= rows) & (cols <= rows + 2 * HALF), 1.0 / (2 * HALF + 1), 0.0
    ).astype(jnp.float32)
    taper = jnp.sin(
        math.pi * (lax.broadcasted_iota(jnp.int32, (NB,), 0).astype(jnp.float32) + 0.5) / NB
    )
    bins = F_LO + lax.broadcasted_iota(jnp.int32, (LAGS, NB), 1)
    lagged = lax.broadcasted_iota(jnp.int32, (LAGS, NB), 0) - LAGS // 2
    angle = (bins * lagged % L).astype(jnp.float32) * (two_pi / L)
    table = jnp.stack([jnp.cos(angle), -jnp.sin(angle)], axis=1).astype(jnp.bfloat16)
    return (smoother, taper, table)


def band_dft(x, f0, nbins, outer=125, prec=lax.Precision.HIGH):
    total, channels = x.shape
    inner = total // outer
    half = outer // 2 + 1
    xb = x.reshape(outer, inner, channels)
    r = lax.broadcasted_iota(jnp.int32, (half, outer), 0)
    b = lax.broadcasted_iota(jnp.int32, (half, outer), 1)
    ang1 = ((r * b) % outer).astype(jnp.float32) * (two_pi / outer)
    basis1 = jnp.concatenate([jnp.cos(ang1), -jnp.sin(ang1)], axis=0)
    z = jnp.einsum("rb,bac->rac", basis1, xb, precision=prec, preferred_element_type=jnp.float32)
    zr, zi = z[:half], z[half:]
    r2 = lax.broadcasted_iota(jnp.int32, (half, inner), 0)
    a2 = lax.broadcasted_iota(jnp.int32, (half, inner), 1)
    ang2 = ((r2 * a2) % total).astype(jnp.float32) * (two_pi / total)
    dc = jnp.cos(ang2)[:, :, None]
    ds = jnp.sin(ang2)[:, :, None]
    wr = dc * zr + ds * zi
    wi = dc * zi - ds * zr
    nj = (f0 + nbins + outer - 1) // outer + 1
    j3 = lax.broadcasted_iota(jnp.int32, (nj, inner), 0)
    a3 = lax.broadcasted_iota(jnp.int32, (nj, inner), 1)
    ang3 = ((j3 * a3) % inner).astype(jnp.float32) * (two_pi / inner)
    basis2 = jnp.concatenate([jnp.cos(ang3), jnp.sin(ang3)], axis=0)
    u = jnp.einsum(
        "ja,srac->sjrc", basis2, jnp.stack([wr, wi]), precision=prec,
        preferred_element_type=jnp.float32,
    )
    u1, u4 = u[0, :nj], u[0, nj:]
    u3, u2 = u[1, :nj], u[1, nj:]
    dre, dim = u1 + u2, u3 - u4
    cre, cim = u1 - u2, -u3 - u4
    f = f0 + lax.broadcasted_iota(jnp.int32, (nbins, nj, half), 0)
    jj = lax.broadcasted_iota(jnp.int32, (nbins, nj, half), 1)
    rr = lax.broadcasted_iota(jnp.int32, (nbins, nj, half), 2)
    direct = (f == outer * jj + rr)
    conj = (f == outer * jj - rr) & (rr > 0) & (f % outer >= half)
    pick = jnp.concatenate([direct, conj], axis=1).astype(jnp.float32).reshape(nbins, 2 * nj * half)
    parts_re = jnp.concatenate([dre, cre], axis=0).reshape(2 * nj * half, channels)
    parts_im = jnp.concatenate([dim, cim], axis=0).reshape(2 * nj * half, channels)
    hi = lax.Precision.HIGHEST
    return jnp.dot(pick, parts_re, precision=hi), jnp.dot(pick, parts_im, precision=hi)


def whiten_local(trace, smoother, taper):
    width = NB + 2 * HALF
    real, imag = band_dft(trace, F_LO - HALF, width)
    power = real * real + imag * imag
    level = jnp.dot(smoother, power, precision=lax.Precision.HIGHEST) + 1e-06
    factor = taper[:, None] * lax.rsqrt(level)
    white = jnp.stack([real[HALF : HALF + NB] * factor, imag[HALF : HALF + NB] * factor])
    return white.astype(jnp.bfloat16)


def cross_spectra(left, right):
    left_re = left[..., 0, :, :].astype(jnp.float32)
    left_im = left[..., 1, :, :].astype(jnp.float32)
    right_re = right[..., 0, :, :].astype(jnp.float32)
    right_im = right[..., 1, :, :].astype(jnp.float32)
    real = left_re * right_re + left_im * right_im
    imag = left_im * right_re - left_re * right_im
    return jnp.stack([real, imag], axis=-3).astype(jnp.bfloat16)


def body(traces, pair_blocks):
    smoother, taper, table = band_tables()
    white = whiten_local(traces[0], smoother, taper)
    nx = lax.axis_size("cx")
    nz = lax.axis_size("cz")
    blocks = nx * nz
    nwin = lax.axis_size("win")
    windows_all = traces.shape[0] * nwin
    factor = 1.0 / math.sqrt(NB * windows_all)
    received = {}
    for shift in (-1, 2):
        perm = [(k + shift, k) for k in range(blocks) if 0 <= k + shift < blocks]
        received[shift] = lax.ppermute(white, ("cx", "cz"), perm)
    left = jnp.stack([received[-1], white, received[-1]])
    right = jnp.stack([white, received[2], received[2]])
    cross = cross_spectra(left, right)
    corr = jnp.einsum("tqb,dqbk->tdk", table, cross, preferred_element_type=jnp.float32) * factor
    lags = corr.shape[0] // nwin
    corr = corr.reshape((nwin, lags) + corr.shape[1:])
    corr = lax.all_to_all(corr, "win", 0, 0).sum(axis=0)
    def shift_z(value, step):
        return lax.ppermute(value, "cz", [(k, (k - step) % nz) for k in range(nz)])

    gathered = {0: corr}
    for step in (1, -1, 2, -2):
        gathered[step % nz] = shift_z(corr, step)
    ahead = shift_z(jnp.stack([gathered[1], gathered[2]]), 2)
    behind = shift_z(gathered[nz - 1], -2)
    gathered[3], gathered[4] = ahead[0], ahead[1]
    gathered[nz - 3] = behind
    ring = jnp.stack([gathered[j] for j in range(nz)])
    me_x = lax.axis_index("cx")
    shifted = [pair_blocks]
    for step in range(1, nx):
        shifted.append(lax.ppermute(pair_blocks, "cx", [(k, (k + step) % nx) for k in range(nx)]))
    shifted = jnp.stack(shifted)
    owners = shifted[(me_x - jnp.arange(nx)) % nx]
    lb = owners[..., 0]
    offset = owners[..., 1] - lb
    filled = lb >= 0
    holder = jnp.where(filled, lb + (offset != 2).astype(jnp.int32), 0)
    mine = filled & (holder // nz == me_x)
    zi = jnp.where(mine, (holder - lax.axis_index("cz")) % nz, 0)
    di = jnp.where(mine, offset - 1, 0)
    picked = ring[zi, :, di, :]
    picked = jnp.where(mine[..., None, None], picked, 0.0)
    got = lax.dynamic_index_in_dim(picked, me_x, 0, keepdims=False)
    for step in range(1, nx):
        chunk = lax.dynamic_index_in_dim(picked, (me_x + step) % nx, 0, keepdims=False)
        got = got + lax.ppermute(chunk, "cx", [(k, (k + step) % nx) for k in range(nx)])
    return jnp.where(filled_local(pair_blocks)[:, None, None], got, 0.0)


def filled_local(pair_blocks):
    return pair_blocks[:, 0] >= 0


def solution(mesh):
    nx = 4
    devices = mesh.devices.reshape(mesh.devices.shape[0], nx, -1)
    grid = jax.sharding.Mesh(devices, ("win", "cx", "cz"))
    in_specs = (P("win", None, ("cx", "cz")), P(("cx", "cz"), None))
    out_specs = P(("cx", "cz"), "win", None)
    return jax.shard_map(body, mesh=grid, in_specs=in_specs, out_specs=out_specs, check_vma=False)
```

```python
import math

import jax
import jax.numpy as jnp
from jax import lax
from jax.sharding import PartitionSpec as P

L = 15000
NB = 512
F_LO = 64
HALF = 32
LAGS = 512
REACH = 3

two_pi = 2.0 * math.pi


def band_tables():
    width = NB + 2 * HALF
    rows = lax.broadcasted_iota(jnp.int32, (NB, width), 0)
    cols = lax.broadcasted_iota(jnp.int32, (NB, width), 1)
    smoother = jnp.where(
        (cols >= rows) & (cols <= rows + 2 * HALF), 1.0 / (2 * HALF + 1), 0.0
    ).astype(jnp.float32)
    taper = jnp.sin(
        math.pi * (lax.broadcasted_iota(jnp.int32, (NB,), 0).astype(jnp.float32) + 0.5) / NB
    )
    bins = F_LO + lax.broadcasted_iota(jnp.int32, (LAGS, NB), 1)
    lagged = lax.broadcasted_iota(jnp.int32, (LAGS, NB), 0) - LAGS // 2
    angle = (bins * lagged % L).astype(jnp.float32) * (two_pi / L)
    table = jnp.stack([jnp.cos(angle), -jnp.sin(angle)], axis=1).astype(jnp.bfloat16)
    return (smoother, taper, table)


def band_dft(x, f0, nbins, outer=125, prec=lax.Precision.HIGH):
    total, channels = x.shape
    inner = total // outer
    half = outer // 2 + 1
    xb = x.reshape(outer, inner, channels)
    r = lax.broadcasted_iota(jnp.int32, (half, outer), 0)
    b = lax.broadcasted_iota(jnp.int32, (half, outer), 1)
    ang1 = ((r * b) % outer).astype(jnp.float32) * (two_pi / outer)
    basis1 = jnp.concatenate([jnp.cos(ang1), -jnp.sin(ang1)], axis=0)
    z = jnp.einsum("rb,bac->rac", basis1, xb, precision=prec, preferred_element_type=jnp.float32)
    zr, zi = z[:half], z[half:]
    r2 = lax.broadcasted_iota(jnp.int32, (half, inner), 0)
    a2 = lax.broadcasted_iota(jnp.int32, (half, inner), 1)
    ang2 = ((r2 * a2) % total).astype(jnp.float32) * (two_pi / total)
    dc = jnp.cos(ang2)[:, :, None]
    ds = jnp.sin(ang2)[:, :, None]
    wr = dc * zr + ds * zi
    wi = dc * zi - ds * zr
    nj = (f0 + nbins + outer - 1) // outer + 1
    j3 = lax.broadcasted_iota(jnp.int32, (nj, inner), 0)
    a3 = lax.broadcasted_iota(jnp.int32, (nj, inner), 1)
    ang3 = ((j3 * a3) % inner).astype(jnp.float32) * (two_pi / inner)
    basis2 = jnp.concatenate([jnp.cos(ang3), jnp.sin(ang3)], axis=0)
    u = jnp.einsum(
        "ja,srac->sjrc", basis2, jnp.stack([wr, wi]), precision=prec,
        preferred_element_type=jnp.float32,
    )
    u1, u4 = u[0, :nj], u[0, nj:]
    u3, u2 = u[1, :nj], u[1, nj:]
    dre, dim = u1 + u2, u3 - u4
    cre, cim = u1 - u2, -u3 - u4
    f = f0 + lax.broadcasted_iota(jnp.int32, (nbins, nj, half), 0)
    jj = lax.broadcasted_iota(jnp.int32, (nbins, nj, half), 1)
    rr = lax.broadcasted_iota(jnp.int32, (nbins, nj, half), 2)
    direct = (f == outer * jj + rr)
    conj = (f == outer * jj - rr) & (rr > 0) & (f % outer >= half)
    pick = jnp.concatenate([direct, conj], axis=1).astype(jnp.float32).reshape(nbins, 2 * nj * half)
    parts_re = jnp.concatenate([dre, cre], axis=0).reshape(2 * nj * half, channels)
    parts_im = jnp.concatenate([dim, cim], axis=0).reshape(2 * nj * half, channels)
    hi = lax.Precision.HIGHEST
    return jnp.dot(pick, parts_re, precision=hi), jnp.dot(pick, parts_im, precision=hi)


def whiten_local(trace, smoother, taper):
    width = NB + 2 * HALF
    real, imag = band_dft(trace, F_LO - HALF, width)
    power = real * real + imag * imag
    level = jnp.dot(smoother, power, precision=lax.Precision.HIGHEST) + 1e-06
    factor = taper[:, None] * lax.rsqrt(level)
    white = jnp.stack([real[HALF : HALF + NB] * factor, imag[HALF : HALF + NB] * factor])
    return white.astype(jnp.bfloat16)


def cross_spectra(left, right):
    left_re = left[..., 0, :, :].astype(jnp.float32)
    left_im = left[..., 1, :, :].astype(jnp.float32)
    right_re = right[..., 0, :, :].astype(jnp.float32)
    right_im = right[..., 1, :, :].astype(jnp.float32)
    real = left_re * right_re + left_im * right_im
    imag = left_im * right_re - left_re * right_im
    return jnp.stack([real, imag], axis=-3).astype(jnp.bfloat16)


def body(traces, pair_blocks):
    smoother, taper, table = band_tables()
    white = whiten_local(traces[0], smoother, taper)
    nx = lax.axis_size("cx")
    nz = lax.axis_size("cz")
    blocks = nx * nz
    nwin = lax.axis_size("win")
    windows_all = traces.shape[0] * nwin
    factor = 1.0 / math.sqrt(NB * windows_all)
    received = {}
    for shift in (-1, 2):
        perm = [(k + shift, k) for k in range(blocks) if 0 <= k + shift < blocks]
        received[shift] = lax.ppermute(white, ("cx", "cz"), perm)
    first = cross_spectra(received[-1][None], white[None])
    rest = cross_spectra(jnp.stack([white, received[-1]]), jnp.stack([received[2], received[2]]))
    lags = LAGS // nwin

    def window_sum(cross):
        corr = jnp.einsum("tqb,dqbk->tdk", table, cross, preferred_element_type=jnp.float32) * factor
        corr = corr.reshape((nwin, lags) + corr.shape[1:])
        return lax.all_to_all(corr, "win", 0, 0).sum(axis=0)

    corr = jnp.concatenate([window_sum(first), window_sum(rest)], axis=1)
    def shift_z(value, step):
        return lax.ppermute(value, "cz", [(k, (k - step) % nz) for k in range(nz)])

    gathered = {0: corr}
    for step in (1, -1, 2, -2):
        gathered[step % nz] = shift_z(corr, step)
    ahead = shift_z(jnp.stack([gathered[1], gathered[2]]), 2)
    behind = shift_z(gathered[nz - 1], -2)
    gathered[3], gathered[4] = ahead[0], ahead[1]
    gathered[nz - 3] = behind
    ring = jnp.stack([gathered[j] for j in range(nz)])
    me_x = lax.axis_index("cx")
    shifted = [pair_blocks]
    for step in range(1, nx):
        shifted.append(lax.ppermute(pair_blocks, "cx", [(k, (k + step) % nx) for k in range(nx)]))
    shifted = jnp.stack(shifted)
    owners = shifted[(me_x - jnp.arange(nx)) % nx]
    lb = owners[..., 0]
    offset = owners[..., 1] - lb
    filled = lb >= 0
    holder = jnp.where(filled, lb + (offset != 2).astype(jnp.int32), 0)
    mine = filled & (holder // nz == me_x)
    zi = jnp.where(mine, (holder - lax.axis_index("cz")) % nz, 0)
    di = jnp.where(mine, offset - 1, 0)
    picked = ring[zi, :, di, :]
    picked = jnp.where(mine[..., None, None], picked, 0.0)
    got = lax.dynamic_index_in_dim(picked, me_x, 0, keepdims=False)
    for step in range(1, nx):
        chunk = lax.dynamic_index_in_dim(picked, (me_x + step) % nx, 0, keepdims=False)
        got = got + lax.ppermute(chunk, "cx", [(k, (k + step) % nx) for k in range(nx)])
    return jnp.where(filled_local(pair_blocks)[:, None, None], got, 0.0)


def filled_local(pair_blocks):
    return pair_blocks[:, 0] >= 0


def solution(mesh):
    nx = 4
    devices = mesh.devices.reshape(mesh.devices.shape[0], nx, -1)
    grid = jax.sharding.Mesh(devices, ("win", "cx", "cz"))
    in_specs = (P("win", None, ("cx", "cz")), P(("cx", "cz"), None))
    out_specs = P(("cx", "cz"), "win", None)
    return jax.shard_map(body, mesh=grid, in_specs=in_specs, out_specs=out_specs, check_vma=False)
```

```python
import math

import jax
import jax.numpy as jnp
from jax import lax
from jax.sharding import PartitionSpec as P

L = 15000
NB = 512
F_LO = 64
HALF = 32
LAGS = 512
REACH = 3

two_pi = 2.0 * math.pi


def band_tables():
    width = NB + 2 * HALF
    rows = lax.broadcasted_iota(jnp.int32, (NB, width), 0)
    cols = lax.broadcasted_iota(jnp.int32, (NB, width), 1)
    smoother = jnp.where(
        (cols >= rows) & (cols <= rows + 2 * HALF), 1.0 / (2 * HALF + 1), 0.0
    ).astype(jnp.float32)
    taper = jnp.sin(
        math.pi * (lax.broadcasted_iota(jnp.int32, (NB,), 0).astype(jnp.float32) + 0.5) / NB
    )
    bins = F_LO + lax.broadcasted_iota(jnp.int32, (LAGS, NB), 1)
    lagged = lax.broadcasted_iota(jnp.int32, (LAGS, NB), 0) - LAGS // 2
    angle = (bins * lagged % L).astype(jnp.float32) * (two_pi / L)
    table = jnp.stack([jnp.cos(angle), -jnp.sin(angle)], axis=1).astype(jnp.bfloat16)
    return (smoother, taper, table)


def band_dft(x, f0, nbins, outer=125, prec=lax.Precision.HIGH):
    total, channels = x.shape
    inner = total // outer
    half = outer // 2 + 1
    xb = x.reshape(outer, inner, channels)
    r = lax.broadcasted_iota(jnp.int32, (half, outer), 0)
    b = lax.broadcasted_iota(jnp.int32, (half, outer), 1)
    ang1 = ((r * b) % outer).astype(jnp.float32) * (two_pi / outer)
    basis1 = jnp.concatenate([jnp.cos(ang1), -jnp.sin(ang1)], axis=0)
    z = jnp.einsum("rb,bac->rac", basis1, xb, precision=prec, preferred_element_type=jnp.float32)
    zr, zi = z[:half], z[half:]
    r2 = lax.broadcasted_iota(jnp.int32, (half, inner), 0)
    a2 = lax.broadcasted_iota(jnp.int32, (half, inner), 1)
    ang2 = ((r2 * a2) % total).astype(jnp.float32) * (two_pi / total)
    dc = jnp.cos(ang2)[:, :, None]
    ds = jnp.sin(ang2)[:, :, None]
    wr = dc * zr + ds * zi
    wi = dc * zi - ds * zr
    nj = (f0 + nbins + outer - 1) // outer + 1
    j3 = lax.broadcasted_iota(jnp.int32, (nj, inner), 0)
    a3 = lax.broadcasted_iota(jnp.int32, (nj, inner), 1)
    ang3 = ((j3 * a3) % inner).astype(jnp.float32) * (two_pi / inner)
    basis2 = jnp.concatenate([jnp.cos(ang3), jnp.sin(ang3)], axis=0)
    u = jnp.einsum(
        "ja,srac->sjrc", basis2, jnp.stack([wr, wi]), precision=prec,
        preferred_element_type=jnp.float32,
    )
    u1, u4 = u[0, :nj], u[0, nj:]
    u3, u2 = u[1, :nj], u[1, nj:]
    dre, dim = u1 + u2, u3 - u4
    cre, cim = u1 - u2, -u3 - u4
    f = f0 + lax.broadcasted_iota(jnp.int32, (nbins, nj, half), 0)
    jj = lax.broadcasted_iota(jnp.int32, (nbins, nj, half), 1)
    rr = lax.broadcasted_iota(jnp.int32, (nbins, nj, half), 2)
    direct = (f == outer * jj + rr)
    conj = (f == outer * jj - rr) & (rr > 0) & (f % outer >= half)
    pick = jnp.concatenate([direct, conj], axis=1).astype(jnp.float32).reshape(nbins, 2 * nj * half)
    parts_re = jnp.concatenate([dre, cre], axis=0).reshape(2 * nj * half, channels)
    parts_im = jnp.concatenate([dim, cim], axis=0).reshape(2 * nj * half, channels)
    hi = lax.Precision.HIGHEST
    return jnp.dot(pick, parts_re, precision=hi), jnp.dot(pick, parts_im, precision=hi)


def whiten_local(trace, smoother, taper):
    width = NB + 2 * HALF
    real, imag = band_dft(trace, F_LO - HALF, width)
    power = real * real + imag * imag
    level = jnp.dot(smoother, power, precision=lax.Precision.HIGHEST) + 1e-06
    factor = taper[:, None] * lax.rsqrt(level)
    white = jnp.stack([real[HALF : HALF + NB] * factor, imag[HALF : HALF + NB] * factor])
    return white.astype(jnp.bfloat16)


def cross_spectra(left, right):
    left_re = left[..., 0, :, :].astype(jnp.float32)
    left_im = left[..., 1, :, :].astype(jnp.float32)
    right_re = right[..., 0, :, :].astype(jnp.float32)
    right_im = right[..., 1, :, :].astype(jnp.float32)
    real = left_re * right_re + left_im * right_im
    imag = left_im * right_re - left_re * right_im
    return jnp.stack([real, imag], axis=-3).astype(jnp.bfloat16)


def body(traces, pair_blocks):
    smoother, taper, table = band_tables()
    white = whiten_local(traces[0], smoother, taper)
    nx = lax.axis_size("cx")
    nz = lax.axis_size("cz")
    blocks = nx * nz
    nwin = lax.axis_size("win")
    windows_all = traces.shape[0] * nwin
    factor = 1.0 / math.sqrt(NB * windows_all)
    def shift_chan(value, step):
        perm = [(k + step, k) for k in range(blocks) if 0 <= k + step < blocks]
        return lax.ppermute(value, ("cx", "cz"), perm)

    before = shift_chan(white, -1)
    after = shift_chan(white, 1)
    further = shift_chan(after, 1)
    left = jnp.stack([before, before, before])
    right = jnp.stack([white, after, further])
    cross = cross_spectra(left, right)
    corr = jnp.einsum("tqb,dqbk->tdk", table, cross, preferred_element_type=jnp.float32) * factor
    lags = corr.shape[0] // nwin
    corr = corr.reshape((nwin, lags) + corr.shape[1:])
    corr = lax.all_to_all(corr, "win", 0, 0).sum(axis=0)
    def shift_z(value, step):
        return lax.ppermute(value, "cz", [(k, (k - step) % nz) for k in range(nz)])

    gathered = {0: corr}
    for step in (1, -1, 2, -2):
        gathered[step % nz] = shift_z(corr, step)
    ahead = shift_z(jnp.stack([gathered[1], gathered[2]]), 2)
    behind = shift_z(gathered[nz - 1], -2)
    gathered[3], gathered[4] = ahead[0], ahead[1]
    gathered[nz - 3] = behind
    ring = jnp.stack([gathered[j] for j in range(nz)])
    me_x = lax.axis_index("cx")
    shifted = [pair_blocks]
    for step in range(1, nx):
        shifted.append(lax.ppermute(pair_blocks, "cx", [(k, (k + step) % nx) for k in range(nx)]))
    shifted = jnp.stack(shifted)
    owners = shifted[(me_x - jnp.arange(nx)) % nx]
    lb = owners[..., 0]
    offset = owners[..., 1] - lb
    filled = lb >= 0
    holder = jnp.where(filled, lb + 1, 0)
    mine = filled & (holder // nz == me_x)
    zi = jnp.where(mine, (holder - lax.axis_index("cz")) % nz, 0)
    di = jnp.where(mine, offset - 1, 0)
    picked = ring[zi, :, di, :]
    picked = jnp.where(mine[..., None, None], picked, 0.0)
    got = lax.dynamic_index_in_dim(picked, me_x, 0, keepdims=False)
    for step in range(1, nx):
        chunk = lax.dynamic_index_in_dim(picked, (me_x + step) % nx, 0, keepdims=False)
        got = got + lax.ppermute(chunk, "cx", [(k, (k + step) % nx) for k in range(nx)])
    return jnp.where(filled_local(pair_blocks)[:, None, None], got, 0.0)


def filled_local(pair_blocks):
    return pair_blocks[:, 0] >= 0


def solution(mesh):
    nx = 4
    devices = mesh.devices.reshape(mesh.devices.shape[0], nx, -1)
    grid = jax.sharding.Mesh(devices, ("win", "cx", "cz"))
    in_specs = (P("win", None, ("cx", "cz")), P(("cx", "cz"), None))
    out_specs = P(("cx", "cz"), "win", None)
    return jax.shard_map(body, mesh=grid, in_specs=in_specs, out_specs=out_specs, check_vma=False)
```

```python
import math

import jax
import jax.numpy as jnp
from jax import lax
from jax.sharding import PartitionSpec as P

L = 15000
NB = 512
F_LO = 64
HALF = 32
LAGS = 512
REACH = 3

two_pi = 2.0 * math.pi


def band_tables():
    width = NB + 2 * HALF
    rows = lax.broadcasted_iota(jnp.int32, (NB, width), 0)
    cols = lax.broadcasted_iota(jnp.int32, (NB, width), 1)
    smoother = jnp.where(
        (cols >= rows) & (cols <= rows + 2 * HALF), 1.0 / (2 * HALF + 1), 0.0
    ).astype(jnp.float32)
    taper = jnp.sin(
        math.pi * (lax.broadcasted_iota(jnp.int32, (NB,), 0).astype(jnp.float32) + 0.5) / NB
    )
    bins = F_LO + lax.broadcasted_iota(jnp.int32, (LAGS, NB), 1)
    lagged = lax.broadcasted_iota(jnp.int32, (LAGS, NB), 0) - LAGS // 2
    angle = (bins * lagged % L).astype(jnp.float32) * (two_pi / L)
    table = jnp.stack([jnp.cos(angle), -jnp.sin(angle)], axis=1).astype(jnp.bfloat16)
    return (smoother, taper, table)


def band_dft(x, f0, nbins, outer=125, prec=lax.Precision.HIGH):
    total, channels = x.shape
    inner = total // outer
    half = outer // 2 + 1
    xb = x.reshape(outer, inner, channels)
    r = lax.broadcasted_iota(jnp.int32, (half, outer), 0)
    b = lax.broadcasted_iota(jnp.int32, (half, outer), 1)
    ang1 = ((r * b) % outer).astype(jnp.float32) * (two_pi / outer)
    basis1 = jnp.concatenate([jnp.cos(ang1), -jnp.sin(ang1)], axis=0)
    z = jnp.einsum("rb,bac->rac", basis1, xb, precision=prec, preferred_element_type=jnp.float32)
    zr, zi = z[:half], z[half:]
    r2 = lax.broadcasted_iota(jnp.int32, (half, inner), 0)
    a2 = lax.broadcasted_iota(jnp.int32, (half, inner), 1)
    ang2 = ((r2 * a2) % total).astype(jnp.float32) * (two_pi / total)
    dc = jnp.cos(ang2)[:, :, None]
    ds = jnp.sin(ang2)[:, :, None]
    wr = dc * zr + ds * zi
    wi = dc * zi - ds * zr
    nj = (f0 + nbins + outer - 1) // outer + 1
    j3 = lax.broadcasted_iota(jnp.int32, (nj, inner), 0)
    a3 = lax.broadcasted_iota(jnp.int32, (nj, inner), 1)
    ang3 = ((j3 * a3) % inner).astype(jnp.float32) * (two_pi / inner)
    basis2 = jnp.concatenate([jnp.cos(ang3), jnp.sin(ang3)], axis=0)
    u = jnp.einsum(
        "ja,srac->sjrc", basis2, jnp.stack([wr, wi]), precision=prec,
        preferred_element_type=jnp.float32,
    )
    u1, u4 = u[0, :nj], u[0, nj:]
    u3, u2 = u[1, :nj], u[1, nj:]
    dre, dim = u1 + u2, u3 - u4
    cre, cim = u1 - u2, -u3 - u4
    f = f0 + lax.broadcasted_iota(jnp.int32, (nbins, nj, half), 0)
    jj = lax.broadcasted_iota(jnp.int32, (nbins, nj, half), 1)
    rr = lax.broadcasted_iota(jnp.int32, (nbins, nj, half), 2)
    direct = (f == outer * jj + rr)
    conj = (f == outer * jj - rr) & (rr > 0) & (f % outer >= half)
    pick = jnp.concatenate([direct, conj], axis=1).astype(jnp.float32).reshape(nbins, 2 * nj * half)
    parts_re = jnp.concatenate([dre, cre], axis=0).reshape(2 * nj * half, channels)
    parts_im = jnp.concatenate([dim, cim], axis=0).reshape(2 * nj * half, channels)
    hi = lax.Precision.HIGHEST
    return jnp.dot(pick, parts_re, precision=hi), jnp.dot(pick, parts_im, precision=hi)


def whiten_local(trace, smoother, taper):
    width = NB + 2 * HALF
    real, imag = band_dft(trace, F_LO - HALF, width)
    power = real * real + imag * imag
    level = jnp.dot(smoother, power, precision=lax.Precision.HIGHEST) + 1e-06
    factor = taper[:, None] * lax.rsqrt(level)
    white = jnp.stack([real[HALF : HALF + NB] * factor, imag[HALF : HALF + NB] * factor])
    return white.astype(jnp.bfloat16)


def cross_spectra(left, right):
    left_re = left[..., 0, :, :].astype(jnp.float32)
    left_im = left[..., 1, :, :].astype(jnp.float32)
    right_re = right[..., 0, :, :].astype(jnp.float32)
    right_im = right[..., 1, :, :].astype(jnp.float32)
    real = left_re * right_re + left_im * right_im
    imag = left_im * right_re - left_re * right_im
    return jnp.stack([real, imag], axis=-3).astype(jnp.bfloat16)


def body(traces, pair_blocks):
    smoother, taper, table = band_tables()
    white = whiten_local(traces[0], smoother, taper)
    nx = lax.axis_size("cx")
    nz = lax.axis_size("cz")
    blocks = nx * nz
    nwin = lax.axis_size("win")
    windows_all = traces.shape[0] * nwin
    factor = 1.0 / math.sqrt(NB * windows_all)
    received = {}
    for shift in (-1, 2):
        perm = [(k + shift, k) for k in range(blocks) if 0 <= k + shift < blocks]
        received[shift] = lax.ppermute(white, ("cx", "cz"), perm)
    left = jnp.stack([received[-1], white, received[-1]])
    right = jnp.stack([white, received[2], received[2]])
    cross = cross_spectra(left, right)
    corr = jnp.einsum("tqb,dqbk->tdk", table, cross, preferred_element_type=jnp.float32) * factor
    lags = corr.shape[0] // nwin
    corr = corr.reshape((nwin, lags) + corr.shape[1:])
    corr = lax.all_to_all(corr.astype(jnp.bfloat16), "win", 0, 0)
    corr = corr.astype(jnp.float32).sum(axis=0)
    def shift_z(value, step):
        return lax.ppermute(value, "cz", [(k, (k - step) % nz) for k in range(nz)])

    gathered = {0: corr}
    for step in (1, -1, 2, -2):
        gathered[step % nz] = shift_z(corr, step)
    ahead = shift_z(jnp.stack([gathered[1], gathered[2]]), 2)
    behind = shift_z(gathered[nz - 1], -2)
    gathered[3], gathered[4] = ahead[0], ahead[1]
    gathered[nz - 3] = behind
    ring = jnp.stack([gathered[j] for j in range(nz)])
    me_x = lax.axis_index("cx")
    shifted = [pair_blocks]
    for step in range(1, nx):
        shifted.append(lax.ppermute(pair_blocks, "cx", [(k, (k + step) % nx) for k in range(nx)]))
    shifted = jnp.stack(shifted)
    owners = shifted[(me_x - jnp.arange(nx)) % nx]
    lb = owners[..., 0]
    offset = owners[..., 1] - lb
    filled = lb >= 0
    holder = jnp.where(filled, lb + (offset != 2).astype(jnp.int32), 0)
    mine = filled & (holder // nz == me_x)
    zi = jnp.where(mine, (holder - lax.axis_index("cz")) % nz, 0)
    di = jnp.where(mine, offset - 1, 0)
    picked = ring[zi, :, di, :]
    picked = jnp.where(mine[..., None, None], picked, 0.0)
    got = lax.dynamic_index_in_dim(picked, me_x, 0, keepdims=False)
    for step in range(1, nx):
        chunk = lax.dynamic_index_in_dim(picked, (me_x + step) % nx, 0, keepdims=False)
        got = got + lax.ppermute(chunk, "cx", [(k, (k + step) % nx) for k in range(nx)])
    return jnp.where(filled_local(pair_blocks)[:, None, None], got, 0.0)


def filled_local(pair_blocks):
    return pair_blocks[:, 0] >= 0


def solution(mesh):
    nx = 4
    devices = mesh.devices.reshape(mesh.devices.shape[0], nx, -1)
    grid = jax.sharding.Mesh(devices, ("win", "cx", "cz"))
    in_specs = (P("win", None, ("cx", "cz")), P(("cx", "cz"), None))
    out_specs = P(("cx", "cz"), "win", None)
    return jax.shard_map(body, mesh=grid, in_specs=in_specs, out_specs=out_specs, check_vma=False)
```

```python
import math

import jax
import jax.numpy as jnp
from jax import lax
from jax.sharding import PartitionSpec as P

L = 15000
NB = 512
F_LO = 64
HALF = 32
LAGS = 512
REACH = 3

two_pi = 2.0 * math.pi


def band_tables():
    width = NB + 2 * HALF
    rows = lax.broadcasted_iota(jnp.int32, (NB, width), 0)
    cols = lax.broadcasted_iota(jnp.int32, (NB, width), 1)
    smoother = jnp.where(
        (cols >= rows) & (cols <= rows + 2 * HALF), 1.0 / (2 * HALF + 1), 0.0
    ).astype(jnp.float32)
    taper = jnp.sin(
        math.pi * (lax.broadcasted_iota(jnp.int32, (NB,), 0).astype(jnp.float32) + 0.5) / NB
    )
    bins = F_LO + lax.broadcasted_iota(jnp.int32, (LAGS, NB), 1)
    lagged = lax.broadcasted_iota(jnp.int32, (LAGS, NB), 0) - LAGS // 2
    angle = (bins * lagged % L).astype(jnp.float32) * (two_pi / L)
    table = jnp.stack([jnp.cos(angle), -jnp.sin(angle)], axis=1).astype(jnp.bfloat16)
    return (smoother, taper, table)


def band_dft(x, f0, nbins, outer=125, prec=lax.Precision.HIGH):
    total, channels = x.shape
    inner = total // outer
    half = outer // 2 + 1
    xb = x.reshape(outer, inner, channels)
    r = lax.broadcasted_iota(jnp.int32, (half, 2, outer), 0)
    part = lax.broadcasted_iota(jnp.int32, (half, 2, outer), 1)
    b = lax.broadcasted_iota(jnp.int32, (half, 2, outer), 2)
    ang1 = ((r * b) % outer).astype(jnp.float32) * (two_pi / outer)
    basis1 = jnp.where(part == 0, jnp.cos(ang1), -jnp.sin(ang1)).reshape(2 * half, outer)
    z = jnp.einsum("rb,bac->rac", basis1, xb, precision=prec, preferred_element_type=jnp.float32)
    z = z.reshape(half, 2, inner, channels)
    nj = (f0 + nbins + outer - 1) // outer + 1
    shape = (half, 2, nj, inner)
    r2 = lax.broadcasted_iota(jnp.int32, shape, 0)
    kind = lax.broadcasted_iota(jnp.int32, shape, 1)
    j2 = lax.broadcasted_iota(jnp.int32, shape, 2)
    a2 = lax.broadcasted_iota(jnp.int32, shape, 3)
    freq = outer * j2 + jnp.where(kind == 0, r2, -r2)
    ang2 = ((a2 * freq) % total).astype(jnp.float32) * (two_pi / total)
    c, s = jnp.cos(ang2), jnp.sin(ang2)
    direct = kind == 0
    m_re = jnp.stack([c, jnp.where(direct, s, -s)], axis=3)
    m_im = jnp.stack([-s, jnp.where(direct, c, -c)], axis=3)
    m = jnp.concatenate([m_re, m_im], axis=1).reshape(half, 4 * nj, 2, inner)
    u = jnp.einsum("rxpa,rpac->rxc", m, z, precision=prec, preferred_element_type=jnp.float32)
    f = f0 + lax.broadcasted_iota(jnp.int32, (nbins, half, 2, nj), 0)
    rr = lax.broadcasted_iota(jnp.int32, (nbins, half, 2, nj), 1)
    kk = lax.broadcasted_iota(jnp.int32, (nbins, half, 2, nj), 2)
    jj = lax.broadcasted_iota(jnp.int32, (nbins, half, 2, nj), 3)
    hit_direct = (kk == 0) & (f == outer * jj + rr)
    hit_conj = (kk == 1) & (f == outer * jj - rr) & (rr > 0) & (f % outer >= half)
    pick = (hit_direct | hit_conj).astype(jnp.float32).reshape(nbins, half * 2 * nj)
    parts_re = u[:, : 2 * nj].reshape(half * 2 * nj, channels)
    parts_im = u[:, 2 * nj :].reshape(half * 2 * nj, channels)
    hi = lax.Precision.HIGHEST
    return jnp.dot(pick, parts_re, precision=hi), jnp.dot(pick, parts_im, precision=hi)


def whiten_local(trace, smoother, taper):
    width = NB + 2 * HALF
    real, imag = band_dft(trace, F_LO - HALF, width)
    power = real * real + imag * imag
    level = jnp.dot(smoother, power, precision=lax.Precision.HIGHEST) + 1e-06
    factor = taper[:, None] * lax.rsqrt(level)
    white = jnp.stack([real[HALF : HALF + NB] * factor, imag[HALF : HALF + NB] * factor])
    return white.astype(jnp.bfloat16)


def cross_spectra(left, right):
    left_re = left[..., 0, :, :].astype(jnp.float32)
    left_im = left[..., 1, :, :].astype(jnp.float32)
    right_re = right[..., 0, :, :].astype(jnp.float32)
    right_im = right[..., 1, :, :].astype(jnp.float32)
    real = left_re * right_re + left_im * right_im
    imag = left_im * right_re - left_re * right_im
    return jnp.stack([real, imag], axis=-3).astype(jnp.bfloat16)


def body(traces, pair_blocks):
    smoother, taper, table = band_tables()
    white = whiten_local(traces[0], smoother, taper)
    nx = lax.axis_size("cx")
    nz = lax.axis_size("cz")
    blocks = nx * nz
    nwin = lax.axis_size("win")
    windows_all = traces.shape[0] * nwin
    factor = 1.0 / math.sqrt(NB * windows_all)
    received = {}
    for shift in (-1, 2):
        perm = [(k + shift, k) for k in range(blocks) if 0 <= k + shift < blocks]
        received[shift] = lax.ppermute(white, ("cx", "cz"), perm)
    left = jnp.stack([received[-1], white, received[-1]])
    right = jnp.stack([white, received[2], received[2]])
    cross = cross_spectra(left, right)
    corr = jnp.einsum("tqb,dqbk->tdk", table, cross, preferred_element_type=jnp.float32) * factor
    lags = corr.shape[0] // nwin
    corr = corr.reshape((nwin, lags) + corr.shape[1:])
    corr = lax.all_to_all(corr.astype(jnp.bfloat16), "win", 0, 0)
    corr = corr.astype(jnp.float32).sum(axis=0)
    def shift_z(value, step):
        return lax.ppermute(value, "cz", [(k, (k - step) % nz) for k in range(nz)])

    gathered = {0: corr}
    for step in (1, -1, 2, -2):
        gathered[step % nz] = shift_z(corr, step)
    ahead = shift_z(jnp.stack([gathered[1], gathered[2]]), 2)
    behind = shift_z(gathered[nz - 1], -2)
    gathered[3], gathered[4] = ahead[0], ahead[1]
    gathered[nz - 3] = behind
    ring = jnp.stack([gathered[j] for j in range(nz)])
    me_x = lax.axis_index("cx")
    shifted = [pair_blocks]
    for step in range(1, nx):
        shifted.append(lax.ppermute(pair_blocks, "cx", [(k, (k + step) % nx) for k in range(nx)]))
    shifted = jnp.stack(shifted)
    owners = shifted[(me_x - jnp.arange(nx)) % nx]
    lb = owners[..., 0]
    offset = owners[..., 1] - lb
    filled = lb >= 0
    holder = jnp.where(filled, lb + (offset != 2).astype(jnp.int32), 0)
    mine = filled & (holder // nz == me_x)
    zi = jnp.where(mine, (holder - lax.axis_index("cz")) % nz, 0)
    di = jnp.where(mine, offset - 1, 0)
    picked = ring[zi, :, di, :]
    picked = jnp.where(mine[..., None, None], picked, 0.0)
    got = lax.dynamic_index_in_dim(picked, me_x, 0, keepdims=False)
    for step in range(1, nx):
        chunk = lax.dynamic_index_in_dim(picked, (me_x + step) % nx, 0, keepdims=False)
        got = got + lax.ppermute(chunk, "cx", [(k, (k + step) % nx) for k in range(nx)])
    return jnp.where(filled_local(pair_blocks)[:, None, None], got, 0.0)


def filled_local(pair_blocks):
    return pair_blocks[:, 0] >= 0


def solution(mesh):
    nx = 4
    devices = mesh.devices.reshape(mesh.devices.shape[0], nx, -1)
    grid = jax.sharding.Mesh(devices, ("win", "cx", "cz"))
    in_specs = (P("win", None, ("cx", "cz")), P(("cx", "cz"), None))
    out_specs = P(("cx", "cz"), "win", None)
    return jax.shard_map(body, mesh=grid, in_specs=in_specs, out_specs=out_specs, check_vma=False)
```

```python
import math

import jax
import jax.numpy as jnp
from jax import lax
from jax.sharding import PartitionSpec as P

L = 15000
NB = 512
F_LO = 64
HALF = 32
LAGS = 512
REACH = 3

two_pi = 2.0 * math.pi


def band_tables():
    width = NB + 2 * HALF
    rows = lax.broadcasted_iota(jnp.int32, (NB, width), 0)
    cols = lax.broadcasted_iota(jnp.int32, (NB, width), 1)
    smoother = jnp.where(
        (cols >= rows) & (cols <= rows + 2 * HALF), 1.0 / (2 * HALF + 1), 0.0
    ).astype(jnp.float32)
    taper = jnp.sin(
        math.pi * (lax.broadcasted_iota(jnp.int32, (NB,), 0).astype(jnp.float32) + 0.5) / NB
    )
    bins = F_LO + lax.broadcasted_iota(jnp.int32, (LAGS, NB), 1)
    lagged = lax.broadcasted_iota(jnp.int32, (LAGS, NB), 0) - LAGS // 2
    angle = (bins * lagged % L).astype(jnp.float32) * (two_pi / L)
    table = jnp.stack([jnp.cos(angle), -jnp.sin(angle)], axis=1).astype(jnp.bfloat16)
    return (smoother, taper, table)


def band_dft(x, f0, nbins, outer=125, prec=lax.Precision.HIGH):
    total, channels = x.shape
    inner = total // outer
    half = outer // 2 + 1
    xb = x.reshape(outer, inner, channels)
    r = lax.broadcasted_iota(jnp.int32, (half, 2, outer), 0)
    part = lax.broadcasted_iota(jnp.int32, (half, 2, outer), 1)
    b = lax.broadcasted_iota(jnp.int32, (half, 2, outer), 2)
    ang1 = ((r * b) % outer).astype(jnp.float32) * (two_pi / outer)
    basis1 = jnp.where(part == 0, jnp.cos(ang1), -jnp.sin(ang1)).reshape(2 * half, outer)
    z = jnp.einsum("rb,bac->rac", basis1, xb, precision=prec, preferred_element_type=jnp.float32)
    z = z.reshape(half, 2, inner, channels)
    nj = (f0 + nbins + outer - 1) // outer
    shape = (half, 2, nj, inner)
    r2 = lax.broadcasted_iota(jnp.int32, shape, 0)
    kind = lax.broadcasted_iota(jnp.int32, shape, 1)
    j2 = lax.broadcasted_iota(jnp.int32, shape, 2)
    a2 = lax.broadcasted_iota(jnp.int32, shape, 3)
    freq = outer * (j2 + kind) + jnp.where(kind == 0, r2, -r2)
    ang2 = ((a2 * freq) % total).astype(jnp.float32) * (two_pi / total)
    c, s = jnp.cos(ang2), jnp.sin(ang2)
    direct = kind == 0
    m_re = jnp.stack([c, jnp.where(direct, s, -s)], axis=3)
    m_im = jnp.stack([-s, jnp.where(direct, c, -c)], axis=3)
    m = jnp.concatenate([m_re, m_im], axis=1).reshape(half, 4 * nj, 2, inner)
    u = jnp.einsum("rxpa,rpac->rxc", m, z, precision=prec, preferred_element_type=jnp.float32)
    f = f0 + lax.broadcasted_iota(jnp.int32, (nbins, half, 2, nj), 0)
    rr = lax.broadcasted_iota(jnp.int32, (nbins, half, 2, nj), 1)
    kk = lax.broadcasted_iota(jnp.int32, (nbins, half, 2, nj), 2)
    jj = lax.broadcasted_iota(jnp.int32, (nbins, half, 2, nj), 3)
    hit_direct = (kk == 0) & (f == outer * jj + rr)
    hit_conj = (kk == 1) & (f == outer * (jj + 1) - rr) & (rr > 0) & (f % outer >= half)
    pick = (hit_direct | hit_conj).astype(jnp.float32).reshape(nbins, half * 2 * nj)
    parts_re = u[:, : 2 * nj].reshape(half * 2 * nj, channels)
    parts_im = u[:, 2 * nj :].reshape(half * 2 * nj, channels)
    hi = lax.Precision.HIGHEST
    return jnp.dot(pick, parts_re, precision=hi), jnp.dot(pick, parts_im, precision=hi)


def whiten_local(trace, smoother, taper):
    width = NB + 2 * HALF
    real, imag = band_dft(trace, F_LO - HALF, width)
    power = real * real + imag * imag
    level = jnp.dot(smoother, power, precision=lax.Precision.HIGHEST) + 1e-06
    factor = taper[:, None] * lax.rsqrt(level)
    white = jnp.stack([real[HALF : HALF + NB] * factor, imag[HALF : HALF + NB] * factor])
    return white.astype(jnp.bfloat16)


def cross_spectra(left, right):
    left_re = left[..., 0, :, :].astype(jnp.float32)
    left_im = left[..., 1, :, :].astype(jnp.float32)
    right_re = right[..., 0, :, :].astype(jnp.float32)
    right_im = right[..., 1, :, :].astype(jnp.float32)
    real = left_re * right_re + left_im * right_im
    imag = left_im * right_re - left_re * right_im
    return jnp.stack([real, imag], axis=-3).astype(jnp.bfloat16)


def body(traces, pair_blocks):
    smoother, taper, table = band_tables()
    white = whiten_local(traces[0], smoother, taper)
    nx = lax.axis_size("cx")
    nz = lax.axis_size("cz")
    blocks = nx * nz
    nwin = lax.axis_size("win")
    windows_all = traces.shape[0] * nwin
    factor = 1.0 / math.sqrt(NB * windows_all)
    received = {}
    for shift in (-1, 2):
        perm = [(k + shift, k) for k in range(blocks) if 0 <= k + shift < blocks]
        received[shift] = lax.ppermute(white, ("cx", "cz"), perm)
    left = jnp.stack([received[-1], white, received[-1]])
    right = jnp.stack([white, received[2], received[2]])
    cross = cross_spectra(left, right)
    corr = jnp.einsum("tqb,dqbk->tdk", table, cross, preferred_element_type=jnp.float32) * factor
    lags = corr.shape[0] // nwin
    corr = corr.reshape((nwin, lags) + corr.shape[1:])
    corr = lax.all_to_all(corr.astype(jnp.bfloat16), "win", 0, 0)
    corr = corr.astype(jnp.float32).sum(axis=0)
    def shift_z(value, step):
        return lax.ppermute(value, "cz", [(k, (k - step) % nz) for k in range(nz)])

    gathered = {0: corr}
    for step in (1, -1, 2, -2):
        gathered[step % nz] = shift_z(corr, step)
    ahead = shift_z(jnp.stack([gathered[1], gathered[2]]), 2)
    behind = shift_z(gathered[nz - 1], -2)
    gathered[3], gathered[4] = ahead[0], ahead[1]
    gathered[nz - 3] = behind
    ring = jnp.stack([gathered[j] for j in range(nz)])
    me_x = lax.axis_index("cx")
    shifted = [pair_blocks]
    for step in range(1, nx):
        shifted.append(lax.ppermute(pair_blocks, "cx", [(k, (k + step) % nx) for k in range(nx)]))
    shifted = jnp.stack(shifted)
    owners = shifted[(me_x - jnp.arange(nx)) % nx]
    lb = owners[..., 0]
    offset = owners[..., 1] - lb
    filled = lb >= 0
    holder = jnp.where(filled, lb + (offset != 2).astype(jnp.int32), 0)
    mine = filled & (holder // nz == me_x)
    zi = jnp.where(mine, (holder - lax.axis_index("cz")) % nz, 0)
    di = jnp.where(mine, offset - 1, 0)
    picked = ring[zi, :, di, :]
    picked = jnp.where(mine[..., None, None], picked, 0.0)
    got = lax.dynamic_index_in_dim(picked, me_x, 0, keepdims=False)
    for step in range(1, nx):
        chunk = lax.dynamic_index_in_dim(picked, (me_x + step) % nx, 0, keepdims=False)
        got = got + lax.ppermute(chunk, "cx", [(k, (k + step) % nx) for k in range(nx)])
    return jnp.where(filled_local(pair_blocks)[:, None, None], got, 0.0)


def filled_local(pair_blocks):
    return pair_blocks[:, 0] >= 0


def solution(mesh):
    nx = 4
    devices = mesh.devices.reshape(mesh.devices.shape[0], nx, -1)
    grid = jax.sharding.Mesh(devices, ("win", "cx", "cz"))
    in_specs = (P("win", None, ("cx", "cz")), P(("cx", "cz"), None))
    out_specs = P(("cx", "cz"), "win", None)
    return jax.shard_map(body, mesh=grid, in_specs=in_specs, out_specs=out_specs, check_vma=False)
```

```python
import math

import jax
import jax.numpy as jnp
from jax import lax
from jax.sharding import PartitionSpec as P

L = 15000
NB = 512
F_LO = 64
HALF = 32
LAGS = 512
REACH = 3

two_pi = 2.0 * math.pi


def band_tables():
    width = NB + 2 * HALF
    rows = lax.broadcasted_iota(jnp.int32, (NB, width), 0)
    cols = lax.broadcasted_iota(jnp.int32, (NB, width), 1)
    smoother = jnp.where(
        (cols >= rows) & (cols <= rows + 2 * HALF), 1.0 / (2 * HALF + 1), 0.0
    ).astype(jnp.float32)
    taper = jnp.sin(
        math.pi * (lax.broadcasted_iota(jnp.int32, (NB,), 0).astype(jnp.float32) + 0.5) / NB
    )
    bins = F_LO + lax.broadcasted_iota(jnp.int32, (LAGS, NB), 1)
    lagged = lax.broadcasted_iota(jnp.int32, (LAGS, NB), 0) - LAGS // 2
    angle = (bins * lagged % L).astype(jnp.float32) * (two_pi / L)
    table = jnp.stack([jnp.cos(angle), -jnp.sin(angle)], axis=1).astype(jnp.bfloat16)
    return (smoother, taper, table)


def band_dft(x, f0, nbins, outer=125, prec=lax.Precision.HIGH):
    total, channels = x.shape
    inner = total // outer
    half = outer // 2 + 1
    xb = x.reshape(outer, inner, channels)
    r = lax.broadcasted_iota(jnp.int32, (half, 2, outer), 0)
    part = lax.broadcasted_iota(jnp.int32, (half, 2, outer), 1)
    b = lax.broadcasted_iota(jnp.int32, (half, 2, outer), 2)
    ang1 = ((r * b) % outer).astype(jnp.float32) * (two_pi / outer)
    basis1 = jnp.where(part == 0, jnp.cos(ang1), -jnp.sin(ang1)).reshape(2 * half, outer)
    z = jnp.einsum("rb,bac->rac", basis1, xb, precision=prec, preferred_element_type=jnp.float32)
    z = z.reshape(half, 2, inner, channels)
    nj = (f0 + nbins + outer - 1) // outer
    shape = (half, 2, nj, inner)
    r2 = lax.broadcasted_iota(jnp.int32, shape, 0)
    kind = lax.broadcasted_iota(jnp.int32, shape, 1)
    j2 = lax.broadcasted_iota(jnp.int32, shape, 2)
    a2 = lax.broadcasted_iota(jnp.int32, shape, 3)
    freq = outer * (j2 + kind) + jnp.where(kind == 0, r2, -r2)
    ang2 = ((a2 * freq) % total).astype(jnp.float32) * (two_pi / total)
    c, s = jnp.cos(ang2), jnp.sin(ang2)
    direct = kind == 0
    m_re = jnp.stack([c, jnp.where(direct, s, -s)], axis=3)
    m_im = jnp.stack([-s, jnp.where(direct, c, -c)], axis=3)
    m = jnp.concatenate([m_re, m_im], axis=1).reshape(half, 4 * nj, 2, inner)
    u = jnp.einsum("rxpa,rpac->rxc", m, z, precision=prec, preferred_element_type=jnp.float32)
    f = f0 + lax.broadcasted_iota(jnp.int32, (nbins, half, 2, nj), 0)
    rr = lax.broadcasted_iota(jnp.int32, (nbins, half, 2, nj), 1)
    kk = lax.broadcasted_iota(jnp.int32, (nbins, half, 2, nj), 2)
    jj = lax.broadcasted_iota(jnp.int32, (nbins, half, 2, nj), 3)
    hit_direct = (kk == 0) & (f == outer * jj + rr)
    hit_conj = (kk == 1) & (f == outer * (jj + 1) - rr) & (rr > 0) & (f % outer >= half)
    pick = (hit_direct | hit_conj).astype(jnp.float32).reshape(nbins, half * 2 * nj)
    parts = jnp.concatenate([u[:, : 2 * nj], u[:, 2 * nj :]], axis=-1)
    both = jnp.dot(pick, parts.reshape(half * 2 * nj, 2 * channels), precision=lax.Precision.HIGHEST)
    return both[:, :channels], both[:, channels:]


def whiten_local(trace, smoother, taper):
    width = NB + 2 * HALF
    real, imag = band_dft(trace, F_LO - HALF, width)
    power = real * real + imag * imag
    level = jnp.dot(smoother, power, precision=lax.Precision.HIGHEST) + 1e-06
    factor = taper[:, None] * lax.rsqrt(level)
    white = jnp.stack([real[HALF : HALF + NB] * factor, imag[HALF : HALF + NB] * factor])
    return white.astype(jnp.bfloat16)


def cross_spectra(left, right):
    left_re = left[..., 0, :, :].astype(jnp.float32)
    left_im = left[..., 1, :, :].astype(jnp.float32)
    right_re = right[..., 0, :, :].astype(jnp.float32)
    right_im = right[..., 1, :, :].astype(jnp.float32)
    real = left_re * right_re + left_im * right_im
    imag = left_im * right_re - left_re * right_im
    return jnp.stack([real, imag], axis=-3).astype(jnp.bfloat16)


def body(traces, pair_blocks):
    smoother, taper, table = band_tables()
    white = whiten_local(traces[0], smoother, taper)
    nx = lax.axis_size("cx")
    nz = lax.axis_size("cz")
    blocks = nx * nz
    nwin = lax.axis_size("win")
    windows_all = traces.shape[0] * nwin
    factor = 1.0 / math.sqrt(NB * windows_all)
    received = {}
    for shift in (-1, 2):
        perm = [(k + shift, k) for k in range(blocks) if 0 <= k + shift < blocks]
        received[shift] = lax.ppermute(white, ("cx", "cz"), perm)
    left = jnp.stack([received[-1], white, received[-1]])
    right = jnp.stack([white, received[2], received[2]])
    cross = cross_spectra(left, right)
    corr = jnp.einsum("tqb,dqbk->tdk", table, cross, preferred_element_type=jnp.float32) * factor
    lags = corr.shape[0] // nwin
    corr = corr.reshape((nwin, lags) + corr.shape[1:])
    corr = lax.all_to_all(corr.astype(jnp.bfloat16), "win", 0, 0)
    corr = corr.astype(jnp.float32).sum(axis=0)
    def shift_z(value, step):
        return lax.ppermute(value, "cz", [(k, (k - step) % nz) for k in range(nz)])

    gathered = {0: corr}
    for step in (1, -1, 2, -2):
        gathered[step % nz] = shift_z(corr, step)
    ahead = shift_z(jnp.stack([gathered[1], gathered[2]]), 2)
    behind = shift_z(gathered[nz - 1], -2)
    gathered[3], gathered[4] = ahead[0], ahead[1]
    gathered[nz - 3] = behind
    ring = jnp.stack([gathered[j] for j in range(nz)])
    me_x = lax.axis_index("cx")
    shifted = [pair_blocks]
    for step in range(1, nx):
        shifted.append(lax.ppermute(pair_blocks, "cx", [(k, (k + step) % nx) for k in range(nx)]))
    shifted = jnp.stack(shifted)
    owners = shifted[(me_x - jnp.arange(nx)) % nx]
    lb = owners[..., 0]
    offset = owners[..., 1] - lb
    filled = lb >= 0
    holder = jnp.where(filled, lb + (offset != 2).astype(jnp.int32), 0)
    mine = filled & (holder // nz == me_x)
    zi = jnp.where(mine, (holder - lax.axis_index("cz")) % nz, 0)
    di = jnp.where(mine, offset - 1, 0)
    picked = ring[zi, :, di, :]
    picked = jnp.where(mine[..., None, None], picked, 0.0)
    got = lax.dynamic_index_in_dim(picked, me_x, 0, keepdims=False)
    for step in range(1, nx):
        chunk = lax.dynamic_index_in_dim(picked, (me_x + step) % nx, 0, keepdims=False)
        got = got + lax.ppermute(chunk, "cx", [(k, (k + step) % nx) for k in range(nx)])
    return jnp.where(filled_local(pair_blocks)[:, None, None], got, 0.0)


def filled_local(pair_blocks):
    return pair_blocks[:, 0] >= 0


def solution(mesh):
    nx = 4
    devices = mesh.devices.reshape(mesh.devices.shape[0], nx, -1)
    grid = jax.sharding.Mesh(devices, ("win", "cx", "cz"))
    in_specs = (P("win", None, ("cx", "cz")), P(("cx", "cz"), None))
    out_specs = P(("cx", "cz"), "win", None)
    return jax.shard_map(body, mesh=grid, in_specs=in_specs, out_specs=out_specs, check_vma=False)
```

```python
import math

import jax
import jax.numpy as jnp
from jax import lax
from jax.sharding import PartitionSpec as P

L = 15000
NB = 512
F_LO = 64
HALF = 32
LAGS = 512
REACH = 3

two_pi = 2.0 * math.pi


def band_tables():
    width = NB + 2 * HALF
    rows = lax.broadcasted_iota(jnp.int32, (NB, width), 0)
    cols = lax.broadcasted_iota(jnp.int32, (NB, width), 1)
    smoother = jnp.where(
        (cols >= rows) & (cols <= rows + 2 * HALF), 1.0 / (2 * HALF + 1), 0.0
    ).astype(jnp.float32)
    taper = jnp.sin(
        math.pi * (lax.broadcasted_iota(jnp.int32, (NB,), 0).astype(jnp.float32) + 0.5) / NB
    )
    bins = F_LO + lax.broadcasted_iota(jnp.int32, (LAGS, NB), 1)
    lagged = lax.broadcasted_iota(jnp.int32, (LAGS, NB), 0) - LAGS // 2
    angle = (bins * lagged % L).astype(jnp.float32) * (two_pi / L)
    table = jnp.stack([jnp.cos(angle), -jnp.sin(angle)], axis=1).astype(jnp.bfloat16)
    return (smoother, taper, table)


def band_dft(x, f0, nbins, outer=125, prec=lax.Precision.HIGH):
    total, channels = x.shape
    inner = total // outer
    half = outer // 2 + 1
    xb = x.reshape(outer, inner, channels)
    r = lax.broadcasted_iota(jnp.int32, (half, 2, outer), 0)
    part = lax.broadcasted_iota(jnp.int32, (half, 2, outer), 1)
    b = lax.broadcasted_iota(jnp.int32, (half, 2, outer), 2)
    ang1 = ((r * b) % outer).astype(jnp.float32) * (two_pi / outer)
    basis1 = jnp.where(part == 0, jnp.cos(ang1), -jnp.sin(ang1)).reshape(2 * half, outer)
    z = jnp.einsum("rb,bac->rac", basis1, xb, precision=prec, preferred_element_type=jnp.float32)
    z = z.reshape(half, 2, inner, channels)
    nj = (f0 + nbins + outer - 1) // outer
    shape = (half, 2, nj, inner)
    r2 = lax.broadcasted_iota(jnp.int32, shape, 0)
    kind = lax.broadcasted_iota(jnp.int32, shape, 1)
    j2 = lax.broadcasted_iota(jnp.int32, shape, 2)
    a2 = lax.broadcasted_iota(jnp.int32, shape, 3)
    freq = outer * (j2 + kind) + jnp.where(kind == 0, r2, -r2)
    ang2 = ((a2 * freq) % total).astype(jnp.float32) * (two_pi / total)
    c, s = jnp.cos(ang2), jnp.sin(ang2)
    direct = kind == 0
    m_re = jnp.stack([c, jnp.where(direct, s, -s)], axis=3)
    m_im = jnp.stack([-s, jnp.where(direct, c, -c)], axis=3)
    m = jnp.concatenate([m_re, m_im], axis=1).reshape(half, 4 * nj, 2, inner)
    u = jnp.einsum("rxpa,rpac->rxc", m, z, precision=prec, preferred_element_type=jnp.float32)
    f = f0 + lax.broadcasted_iota(jnp.int32, (nbins, half, 2, nj), 0)
    rr = lax.broadcasted_iota(jnp.int32, (nbins, half, 2, nj), 1)
    kk = lax.broadcasted_iota(jnp.int32, (nbins, half, 2, nj), 2)
    jj = lax.broadcasted_iota(jnp.int32, (nbins, half, 2, nj), 3)
    hit_direct = (kk == 0) & (f == outer * jj + rr)
    hit_conj = (kk == 1) & (f == outer * (jj + 1) - rr) & (rr > 0) & (f % outer >= half)
    pick = (hit_direct | hit_conj).astype(jnp.float32).reshape(nbins, half * 2 * nj)
    parts = jnp.concatenate([u[:, : 2 * nj], u[:, 2 * nj :]], axis=-1)
    both = jnp.dot(pick, parts.reshape(half * 2 * nj, 2 * channels), precision=lax.Precision.HIGHEST)
    return both[:, :channels], both[:, channels:]


def whiten_local(trace, smoother, taper):
    width = NB + 2 * HALF
    real, imag = band_dft(trace, F_LO - HALF, width)
    power = real * real + imag * imag
    level = jnp.dot(smoother, power, precision=lax.Precision.HIGHEST) + 1e-06
    factor = taper[:, None] * lax.rsqrt(level)
    white = jnp.stack([real[HALF : HALF + NB] * factor, imag[HALF : HALF + NB] * factor])
    return white.astype(jnp.bfloat16)


def cross_spectra(left, right):
    left_re = left[..., 0, :, :].astype(jnp.float32)
    left_im = left[..., 1, :, :].astype(jnp.float32)
    right_re = right[..., 0, :, :].astype(jnp.float32)
    right_im = right[..., 1, :, :].astype(jnp.float32)
    real = left_re * right_re + left_im * right_im
    imag = left_im * right_re - left_re * right_im
    return jnp.stack([real, imag], axis=-3).astype(jnp.bfloat16)


def body(traces, pair_blocks):
    smoother, taper, table = band_tables()
    white = whiten_local(traces[0], smoother, taper)
    nx = lax.axis_size("cx")
    nz = lax.axis_size("cz")
    blocks = nx * nz
    nwin = lax.axis_size("win")
    windows_all = traces.shape[0] * nwin
    factor = 1.0 / math.sqrt(NB * windows_all)
    received = {}
    for shift in (2, -1):
        perm = [(k + shift, k) for k in range(blocks) if 0 <= k + shift < blocks]
        received[shift] = lax.ppermute(white, ("cx", "cz"), perm)
    left = jnp.stack([received[-1], white, received[-1]])
    right = jnp.stack([white, received[2], received[2]])
    cross = cross_spectra(left, right)
    corr = jnp.einsum("tqb,dqbk->tdk", table, cross, preferred_element_type=jnp.float32) * factor
    lags = corr.shape[0] // nwin
    corr = corr.reshape((nwin, lags) + corr.shape[1:])
    corr = lax.all_to_all(corr.astype(jnp.bfloat16), "win", 0, 0)
    corr = corr.astype(jnp.float32).sum(axis=0)
    def shift_z(value, step):
        return lax.ppermute(value, "cz", [(k, (k - step) % nz) for k in range(nz)])

    gathered = {0: corr}
    for step in (2, -2, 1, -1):
        gathered[step % nz] = shift_z(corr, step)
    ahead = shift_z(jnp.stack([gathered[1], gathered[2]]), 2)
    behind = shift_z(gathered[nz - 1], -2)
    gathered[3], gathered[4] = ahead[0], ahead[1]
    gathered[nz - 3] = behind
    ring = jnp.stack([gathered[j] for j in range(nz)])
    me_x = lax.axis_index("cx")
    shifted = [pair_blocks]
    for step in range(1, nx):
        shifted.append(lax.ppermute(pair_blocks, "cx", [(k, (k + step) % nx) for k in range(nx)]))
    shifted = jnp.stack(shifted)
    owners = shifted[(me_x - jnp.arange(nx)) % nx]
    lb = owners[..., 0]
    offset = owners[..., 1] - lb
    filled = lb >= 0
    holder = jnp.where(filled, lb + (offset != 2).astype(jnp.int32), 0)
    mine = filled & (holder // nz == me_x)
    zi = jnp.where(mine, (holder - lax.axis_index("cz")) % nz, 0)
    di = jnp.where(mine, offset - 1, 0)
    picked = ring[zi, :, di, :]
    picked = jnp.where(mine[..., None, None], picked, 0.0)
    got = lax.dynamic_index_in_dim(picked, me_x, 0, keepdims=False)
    for step in sorted(range(1, nx), key=lambda t: -min(t, nx - t)):
        chunk = lax.dynamic_index_in_dim(picked, (me_x + step) % nx, 0, keepdims=False)
        got = got + lax.ppermute(chunk, "cx", [(k, (k + step) % nx) for k in range(nx)])
    return jnp.where(filled_local(pair_blocks)[:, None, None], got, 0.0)


def filled_local(pair_blocks):
    return pair_blocks[:, 0] >= 0


def solution(mesh):
    nx = 4
    devices = mesh.devices.reshape(mesh.devices.shape[0], nx, -1)
    grid = jax.sharding.Mesh(devices, ("win", "cx", "cz"))
    in_specs = (P("win", None, ("cx", "cz")), P(("cx", "cz"), None))
    out_specs = P(("cx", "cz"), "win", None)
    return jax.shard_map(body, mesh=grid, in_specs=in_specs, out_specs=out_specs, check_vma=False)
```

```python
import math

import jax
import jax.numpy as jnp
from jax import lax
from jax.sharding import PartitionSpec as P

L = 15000
NB = 512
F_LO = 64
HALF = 32
LAGS = 512
REACH = 3

two_pi = 2.0 * math.pi


def band_tables():
    width = NB + 2 * HALF
    rows = lax.broadcasted_iota(jnp.int32, (NB, width), 0)
    cols = lax.broadcasted_iota(jnp.int32, (NB, width), 1)
    smoother = jnp.where(
        (cols >= rows) & (cols <= rows + 2 * HALF), 1.0 / (2 * HALF + 1), 0.0
    ).astype(jnp.float32)
    taper = jnp.sin(
        math.pi * (lax.broadcasted_iota(jnp.int32, (NB,), 0).astype(jnp.float32) + 0.5) / NB
    )
    bins = F_LO + lax.broadcasted_iota(jnp.int32, (LAGS, NB), 1)
    lagged = lax.broadcasted_iota(jnp.int32, (LAGS, NB), 0) - LAGS // 2
    angle = (bins * lagged % L).astype(jnp.float32) * (two_pi / L)
    table = jnp.stack([jnp.cos(angle), -jnp.sin(angle)], axis=1).astype(jnp.bfloat16)
    return (smoother, taper, table)


def band_dft(x, f0, nbins, outer=125, prec=lax.Precision.HIGH):
    total, channels = x.shape
    inner = total // outer
    half = outer // 2 + 1
    xb = x.reshape(outer, inner, channels)
    r = lax.broadcasted_iota(jnp.int32, (half, 2, outer), 0)
    part = lax.broadcasted_iota(jnp.int32, (half, 2, outer), 1)
    b = lax.broadcasted_iota(jnp.int32, (half, 2, outer), 2)
    ang1 = ((r * b) % outer).astype(jnp.float32) * (two_pi / outer)
    basis1 = jnp.where(part == 0, jnp.cos(ang1), -jnp.sin(ang1)).reshape(2 * half, outer)
    z = jnp.einsum("rb,bac->rac", basis1, xb, precision=prec, preferred_element_type=jnp.float32)
    z = z.reshape(half, 2, inner, channels)
    nj = (f0 + nbins + outer - 1) // outer
    shape = (half, 2, nj, inner)
    r2 = lax.broadcasted_iota(jnp.int32, shape, 0)
    kind = lax.broadcasted_iota(jnp.int32, shape, 1)
    j2 = lax.broadcasted_iota(jnp.int32, shape, 2)
    a2 = lax.broadcasted_iota(jnp.int32, shape, 3)
    freq = outer * (j2 + kind) + jnp.where(kind == 0, r2, -r2)
    ang2 = ((a2 * freq) % total).astype(jnp.float32) * (two_pi / total)
    c, s = jnp.cos(ang2), jnp.sin(ang2)
    direct = kind == 0
    m_re = jnp.stack([c, jnp.where(direct, s, -s)], axis=3)
    m_im = jnp.stack([-s, jnp.where(direct, c, -c)], axis=3)
    m = jnp.concatenate([m_re, m_im], axis=1).reshape(half, 4 * nj, 2, inner)
    u = jnp.einsum("rxpa,rpac->rxc", m, z, precision=prec, preferred_element_type=jnp.float32)
    f = f0 + lax.broadcasted_iota(jnp.int32, (nbins, half, 2, nj), 0)
    rr = lax.broadcasted_iota(jnp.int32, (nbins, half, 2, nj), 1)
    kk = lax.broadcasted_iota(jnp.int32, (nbins, half, 2, nj), 2)
    jj = lax.broadcasted_iota(jnp.int32, (nbins, half, 2, nj), 3)
    hit_direct = (kk == 0) & (f == outer * jj + rr)
    hit_conj = (kk == 1) & (f == outer * (jj + 1) - rr) & (rr > 0) & (f % outer >= half)
    pick = (hit_direct | hit_conj).astype(jnp.float32).reshape(nbins, half * 2 * nj)
    parts = jnp.concatenate([u[:, : 2 * nj], u[:, 2 * nj :]], axis=-1)
    both = jnp.dot(pick, parts.reshape(half * 2 * nj, 2 * channels), precision=lax.Precision.HIGHEST)
    return both[:, :channels], both[:, channels:]


def whiten_local(trace, smoother, taper):
    width = NB + 2 * HALF
    real, imag = band_dft(trace, F_LO - HALF, width)
    power = real * real + imag * imag
    level = jnp.dot(smoother, power, precision=lax.Precision.HIGHEST) + 1e-06
    factor = taper[:, None] * lax.rsqrt(level)
    white = jnp.stack([real[HALF : HALF + NB] * factor, imag[HALF : HALF + NB] * factor])
    return white.astype(jnp.bfloat16)


def cross_spectra(left, right):
    left_re = left[..., 0, :, :].astype(jnp.float32)
    left_im = left[..., 1, :, :].astype(jnp.float32)
    right_re = right[..., 0, :, :].astype(jnp.float32)
    right_im = right[..., 1, :, :].astype(jnp.float32)
    real = left_re * right_re + left_im * right_im
    imag = left_im * right_re - left_re * right_im
    return jnp.stack([real, imag], axis=-3).astype(jnp.bfloat16)


def body(traces, pair_blocks):
    smoother, taper, table = band_tables()
    white = whiten_local(traces[0], smoother, taper)
    nx = lax.axis_size("cx")
    nz = lax.axis_size("cz")
    blocks = nx * nz
    nwin = lax.axis_size("win")
    windows_all = traces.shape[0] * nwin
    factor = 1.0 / math.sqrt(NB * windows_all)
    received = {}
    for shift in (2, -1):
        perm = [(k + shift, k) for k in range(blocks) if 0 <= k + shift < blocks]
        received[shift] = lax.ppermute(white, ("cx", "cz"), perm)
    left = jnp.stack([received[-1], white, received[-1]])
    right = jnp.stack([white, received[2], received[2]])
    cross = cross_spectra(left, right)
    corr = jnp.einsum("tqb,dqbk->tdk", table, cross, preferred_element_type=jnp.float32) * factor
    lags = corr.shape[0] // nwin
    corr = corr.reshape((nwin, lags) + corr.shape[1:])
    corr = lax.all_to_all(corr.astype(jnp.bfloat16), "win", 0, 0)
    corr = corr.astype(jnp.float32).sum(axis=0)
    def shift_z(value, step):
        return lax.ppermute(value, "cz", [(k, (k - step) % nz) for k in range(nz)])

    gathered = {0: corr}
    for step in (2, -2, 1, -1):
        gathered[step % nz] = shift_z(corr, step)
    gathered[4] = shift_z(gathered[2], 2)
    gathered[3] = shift_z(gathered[2], 1)
    gathered[nz - 3] = shift_z(gathered[nz - 2], -1)
    ring = jnp.stack([gathered[j] for j in range(nz)])
    me_x = lax.axis_index("cx")
    shifted = [pair_blocks]
    for step in range(1, nx):
        shifted.append(lax.ppermute(pair_blocks, "cx", [(k, (k + step) % nx) for k in range(nx)]))
    shifted = jnp.stack(shifted)
    owners = shifted[(me_x - jnp.arange(nx)) % nx]
    lb = owners[..., 0]
    offset = owners[..., 1] - lb
    filled = lb >= 0
    holder = jnp.where(filled, lb + (offset != 2).astype(jnp.int32), 0)
    mine = filled & (holder // nz == me_x)
    zi = jnp.where(mine, (holder - lax.axis_index("cz")) % nz, 0)
    di = jnp.where(mine, offset - 1, 0)
    picked = ring[zi, :, di, :]
    picked = jnp.where(mine[..., None, None], picked, 0.0)
    got = lax.dynamic_index_in_dim(picked, me_x, 0, keepdims=False)
    for step in sorted(range(1, nx), key=lambda t: -min(t, nx - t)):
        chunk = lax.dynamic_index_in_dim(picked, (me_x + step) % nx, 0, keepdims=False)
        got = got + lax.ppermute(chunk, "cx", [(k, (k + step) % nx) for k in range(nx)])
    return jnp.where(filled_local(pair_blocks)[:, None, None], got, 0.0)


def filled_local(pair_blocks):
    return pair_blocks[:, 0] >= 0


def solution(mesh):
    nx = 4
    devices = mesh.devices.reshape(mesh.devices.shape[0], nx, -1)
    grid = jax.sharding.Mesh(devices, ("win", "cx", "cz"))
    in_specs = (P("win", None, ("cx", "cz")), P(("cx", "cz"), None))
    out_specs = P(("cx", "cz"), "win", None)
    return jax.shard_map(body, mesh=grid, in_specs=in_specs, out_specs=out_specs, check_vma=False)
```

```python
import math

import jax
import jax.numpy as jnp
from jax import lax
from jax.sharding import PartitionSpec as P

L = 15000
NB = 512
F_LO = 64
HALF = 32
LAGS = 512
REACH = 3

two_pi = 2.0 * math.pi


def band_tables():
    width = NB + 2 * HALF
    rows = lax.broadcasted_iota(jnp.int32, (NB, width), 0)
    cols = lax.broadcasted_iota(jnp.int32, (NB, width), 1)
    smoother = jnp.where((cols >= rows) & (cols <= rows + 2 * HALF), 1.0, 0.0).astype(jnp.float32)
    taper = jnp.sin(
        math.pi * (lax.broadcasted_iota(jnp.int32, (NB,), 0).astype(jnp.float32) + 0.5) / NB
    )
    bins = F_LO + lax.broadcasted_iota(jnp.int32, (LAGS, NB), 1)
    lagged = lax.broadcasted_iota(jnp.int32, (LAGS, NB), 0) - LAGS // 2
    angle = (bins * lagged % L).astype(jnp.float32) * (two_pi / L)
    table = jnp.stack([jnp.cos(angle), -jnp.sin(angle)], axis=1).astype(jnp.bfloat16)
    return (smoother, taper, table)


def band_dft(x, f0, nbins, outer=125, prec=lax.Precision.HIGH):
    total, channels = x.shape
    inner = total // outer
    half = outer // 2 + 1
    xb = x.reshape(outer, inner, channels)
    r = lax.broadcasted_iota(jnp.int32, (half, 2, outer), 0)
    part = lax.broadcasted_iota(jnp.int32, (half, 2, outer), 1)
    b = lax.broadcasted_iota(jnp.int32, (half, 2, outer), 2)
    ang1 = ((r * b) % outer).astype(jnp.float32) * (two_pi / outer)
    basis1 = jnp.where(part == 0, jnp.cos(ang1), -jnp.sin(ang1)).reshape(2 * half, outer)
    z = jnp.einsum("rb,bac->rac", basis1, xb, precision=prec, preferred_element_type=jnp.float32)
    z = z.reshape(half, 2, inner, channels)
    nj = (f0 + nbins + outer - 1) // outer
    shape = (half, 2, nj, inner)
    r2 = lax.broadcasted_iota(jnp.int32, shape, 0)
    kind = lax.broadcasted_iota(jnp.int32, shape, 1)
    j2 = lax.broadcasted_iota(jnp.int32, shape, 2)
    a2 = lax.broadcasted_iota(jnp.int32, shape, 3)
    freq = outer * (j2 + kind) + jnp.where(kind == 0, r2, -r2)
    ang2 = ((a2 * freq) % total).astype(jnp.float32) * (two_pi / total)
    c, s = jnp.cos(ang2), jnp.sin(ang2)
    direct = kind == 0
    m_re = jnp.stack([c, jnp.where(direct, s, -s)], axis=3)
    m_im = jnp.stack([-s, jnp.where(direct, c, -c)], axis=3)
    m = jnp.concatenate([m_re, m_im], axis=1).reshape(half, 4 * nj, 2, inner)
    u = jnp.einsum("rxpa,rpac->rxc", m, z, precision=prec, preferred_element_type=jnp.float32)
    f = f0 + lax.broadcasted_iota(jnp.int32, (nbins, half, 2, nj), 0)
    rr = lax.broadcasted_iota(jnp.int32, (nbins, half, 2, nj), 1)
    kk = lax.broadcasted_iota(jnp.int32, (nbins, half, 2, nj), 2)
    jj = lax.broadcasted_iota(jnp.int32, (nbins, half, 2, nj), 3)
    hit_direct = (kk == 0) & (f == outer * jj + rr)
    hit_conj = (kk == 1) & (f == outer * (jj + 1) - rr) & (rr > 0) & (f % outer >= half)
    pick = (hit_direct | hit_conj).astype(jnp.float32).reshape(nbins, half * 2 * nj)
    parts = jnp.concatenate([u[:, : 2 * nj], u[:, 2 * nj :]], axis=-1)
    both = jnp.dot(pick, parts.reshape(half * 2 * nj, 2 * channels), precision=lax.Precision.HIGHEST)
    return both[:, :channels], both[:, channels:]


def whiten_local(trace, smoother, taper):
    width = NB + 2 * HALF
    real, imag = band_dft(trace, F_LO - HALF, width)
    power = real * real + imag * imag
    level = jnp.dot(smoother, power, precision=lax.Precision.HIGH) * (1.0 / (2 * HALF + 1)) + 1e-06
    factor = taper[:, None] * lax.rsqrt(level)
    white = jnp.stack([real[HALF : HALF + NB] * factor, imag[HALF : HALF + NB] * factor])
    return white.astype(jnp.bfloat16)


def cross_spectra(left, right):
    left_re = left[..., 0, :, :].astype(jnp.float32)
    left_im = left[..., 1, :, :].astype(jnp.float32)
    right_re = right[..., 0, :, :].astype(jnp.float32)
    right_im = right[..., 1, :, :].astype(jnp.float32)
    real = left_re * right_re + left_im * right_im
    imag = left_im * right_re - left_re * right_im
    return jnp.stack([real, imag], axis=-3).astype(jnp.bfloat16)


def body(traces, pair_blocks):
    smoother, taper, table = band_tables()
    white = whiten_local(traces[0], smoother, taper)
    nx = lax.axis_size("cx")
    nz = lax.axis_size("cz")
    blocks = nx * nz
    nwin = lax.axis_size("win")
    windows_all = traces.shape[0] * nwin
    factor = 1.0 / math.sqrt(NB * windows_all)
    received = {}
    for shift in (2, -1):
        perm = [(k + shift, k) for k in range(blocks) if 0 <= k + shift < blocks]
        received[shift] = lax.ppermute(white, ("cx", "cz"), perm)
    left = jnp.stack([received[-1], white, received[-1]])
    right = jnp.stack([white, received[2], received[2]])
    cross = cross_spectra(left, right)
    corr = jnp.einsum("tqb,dqbk->tdk", table, cross, preferred_element_type=jnp.float32) * factor
    lags = corr.shape[0] // nwin
    corr = corr.reshape((nwin, lags) + corr.shape[1:])
    corr = lax.all_to_all(corr.astype(jnp.bfloat16), "win", 0, 0)
    corr = corr.astype(jnp.float32).sum(axis=0)
    def shift_z(value, step):
        return lax.ppermute(value, "cz", [(k, (k - step) % nz) for k in range(nz)])

    gathered = {0: corr}
    for step in (2, -2, 1, -1):
        gathered[step % nz] = shift_z(corr, step)
    gathered[4] = shift_z(gathered[2], 2)
    gathered[3] = shift_z(gathered[2], 1)
    gathered[nz - 3] = shift_z(gathered[nz - 2], -1)
    ring = jnp.stack([gathered[j] for j in range(nz)])
    me_x = lax.axis_index("cx")
    shifted = [pair_blocks]
    for step in range(1, nx):
        shifted.append(lax.ppermute(pair_blocks, "cx", [(k, (k + step) % nx) for k in range(nx)]))
    shifted = jnp.stack(shifted)
    owners = shifted[(me_x - jnp.arange(nx)) % nx]
    lb = owners[..., 0]
    offset = owners[..., 1] - lb
    filled = lb >= 0
    holder = jnp.where(filled, lb + (offset != 2).astype(jnp.int32), 0)
    mine = filled & (holder // nz == me_x)
    zi = jnp.where(mine, (holder - lax.axis_index("cz")) % nz, 0)
    di = jnp.where(mine, offset - 1, 0)
    picked = ring[zi, :, di, :]
    picked = jnp.where(mine[..., None, None], picked, 0.0)
    got = lax.dynamic_index_in_dim(picked, me_x, 0, keepdims=False)
    for step in sorted(range(1, nx), key=lambda t: -min(t, nx - t)):
        chunk = lax.dynamic_index_in_dim(picked, (me_x + step) % nx, 0, keepdims=False)
        got = got + lax.ppermute(chunk, "cx", [(k, (k + step) % nx) for k in range(nx)])
    return jnp.where(filled_local(pair_blocks)[:, None, None], got, 0.0)


def filled_local(pair_blocks):
    return pair_blocks[:, 0] >= 0


def solution(mesh):
    nx = 4
    devices = mesh.devices.reshape(mesh.devices.shape[0], nx, -1)
    grid = jax.sharding.Mesh(devices, ("win", "cx", "cz"))
    in_specs = (P("win", None, ("cx", "cz")), P(("cx", "cz"), None))
    out_specs = P(("cx", "cz"), "win", None)
    return jax.shard_map(body, mesh=grid, in_specs=in_specs, out_specs=out_specs, check_vma=False)
```
